512 devices in a mesh: tiles: 512 (over y, x, z, core).
Axes of the slice: x: 4, y: 8, z: 8, core: 2. Of those that a mesh axis runs over, the one named last changes fastest.
Arguments:
- fields: bfloat16 [512, 96, 256], P('tiles'), may hold values from -6 to 6
- conv_a: bfloat16 [9, 96, 96], replicated, may hold values from -0.21875 to 0.21875
- bias_a: float32 [96], replicated, may hold values from -3 to 3
- conv_b: bfloat16 [9, 96, 96], replicated, may hold values from -0.21875 to 0.21875
- cotangent: bfloat16 [512, 96, 256], P('tiles'), may hold values from -6 to 6
- neighbour_tile: int32 [512, 4], P('tiles'), may hold values from 0 to 511, as said below
- edge_code: int32 [512, 4], P('tiles'), may hold values from 0 to 7, as said below
- corner_tile: int32 [512, 4], P('tiles'), may hold values from 0 to 511, as said below
- corner_code: int32 [512, 4], P('tiles'), may hold values from 0 to 3, as said below
- corner_missing: int32 [512, 4], P('tiles'), may hold values 0 or 1
Outputs:
- output: bfloat16 [512, 96, 256], P('tiles')
- grad_fields: bfloat16 [512, 96, 256], P('tiles')
- grad_a: float32 [9, 96, 96], replicated
- grad_b: float32 [9, 96, 96], replicated
- grad_bias: float32 [96], replicated
The draws below stay inside these ranges and needn't reach their ends.
Inputs may be any that keep to these rules, and one draw needn't show every extreme that they name: `neighbour_tile`: the atlas is a torus of rows of 8 tiles. The tiles of side k of tile p and of corner c are p plus one of -8, 1, 8, -1 (sides) and of 1 - 8, 9, 7, -1 - 8 (corners), modulo 512, a different offset for each side and each corner of a tile. `edge_code`: adjacency is mutual: if side k of tile p meets side j of tile q, then side j of q meets side k of p, with the same reversal. `corner_tile`: offsets as stated for neighbour_tile. `corner_code`: if corner c of tile p meets corner m of tile q, then corner m of q meets corner c of p.
All inputs are finite; a program needn't handle non-finite values. No bound on the sum of `corner_missing` on one device may be relied on, other than what follows from the above.
Results may differ from the reference program's by a relative error of at most 0.0075.
Values may be sent and summed in bfloat16 or wider, within the bound.
No kernel may reach another device: no remote copies, remote signals or barrier semaphores. Data moves between devices by JAX's collectives and lax.ppermute only.
A program may use at most 64 MiB of HBM per device.

```python
import jax
import jax.numpy as jnp
from jax import lax

C = 96
SIDE = 16
TILE_ROW = 8
TILES = 512


def tile_atlas(key):
    quarter_turn = jax.random.randint(jax.random.fold_in(key, 11), (TILES,), 0, 4)
    offsets = jnp.array([-TILE_ROW, 1, TILE_ROW, -1], dtype=jnp.int32)
    tile_ids = jnp.arange(TILES, dtype=jnp.int32)[:, None]
    side_ids = jnp.arange(4, dtype=jnp.int32)[None, :]
    own_turn = quarter_turn[:, None]
    facing = (side_ids + own_turn) % 4
    neighbour = (tile_ids + offsets[facing]) % TILES
    other_turn = quarter_turn[neighbour]
    other_side = (facing + 2 - other_turn) % 4
    own_run = (1 + side_ids % 2 + own_turn) % 4
    other_run = (1 + other_side % 2 + other_turn) % 4
    edge_codes = other_side + 4 * (own_run != other_run).astype(jnp.int32)
    before = (side_ids + 3 + own_turn) % 4
    diagonal = (tile_ids + offsets[before] + offsets[facing]) % TILES
    corner_codes = (side_ids + 2 + own_turn - quarter_turn[diagonal]) % 4
    return (neighbour, edge_codes, diagonal, corner_codes)


def draw_neighbour_tile(key, part):
    return tile_atlas(key)[0]


def draw_edge_code(key, part):
    return tile_atlas(key)[1]


def draw_corner_tile(key, part):
    return tile_atlas(key)[2]


def draw_corner_code(key, part):
    return tile_atlas(key)[3]


def with_ends(values, key, least, high):
    longest = values.shape.index(max(values.shape))
    spots = []
    for shift in (0, 1):
        where = [jax.random.randint(jax.random.fold_in(key, axis), (), 0, length) for axis, length in enumerate(values.shape)]
        where[longest] = (where[longest] + shift) % values.shape[longest]
        spots.append(tuple(where))
    return values.at[spots[0]].set(least).at[spots[1]].set(high)


def block_levels(key, shape, pieces, least, largest):
    level, own = 1.0, jax.random.fold_in(key, 6)
    for axis_at, blocks in pieces:
        draws = jnp.exp(jax.random.uniform(jax.random.fold_in(own, axis_at), (blocks,), jnp.float32, least / len(pieces), largest / len(pieces)))
        level = level * jnp.repeat(draws, shape[axis_at] // blocks).reshape([-1 if axis == axis_at else 1 for axis in range(len(shape))])
    return level


def scatter_about(own_key, shape, spread, limit, pieces=(), held_as=jnp.bfloat16):
    gain = block_levels(own_key, shape, pieces, -0.22, 0.18) if pieces else 1.0
    drawn = jax.random.normal(own_key, shape, jnp.float32) * spread * gain
    return jnp.minimum(jnp.maximum(drawn, -limit), limit).astype(held_as)


def setup_inputs(seed: int = 0) -> dict:
    key_list = jax.random.split(jax.random.key(seed), 11)
    return {
        "fields": scatter_about(key_list[0], (TILES, C, SIDE * SIDE), 1.0, 6.0, ((0, 512),)),
        "conv_a": scatter_about(key_list[1], (9, C, C), (9 * C) ** -0.5, 0.21875),
        "bias_a": scatter_about(key_list[2], (C,), 0.5, 3.0, (), jnp.float32),
        "conv_b": scatter_about(key_list[3], (9, C, C), (9 * C) ** -0.5, 0.21875),
        "cotangent": scatter_about(key_list[4], (TILES, C, SIDE * SIDE), 1.0, 6.0, ((0, 512),)),
        "neighbour_tile": draw_neighbour_tile(jax.random.fold_in(key_list[10], 71), 0),
        "edge_code": draw_edge_code(jax.random.fold_in(key_list[10], 71), 0),
        "corner_tile": draw_corner_tile(jax.random.fold_in(key_list[10], 71), 0),
        "corner_code": draw_corner_code(jax.random.fold_in(key_list[10], 71), 0),
        "corner_missing": with_ends((jax.random.randint(key_list[9], (TILES, 4), 0, 4) < 1).astype(jnp.int32), jax.random.fold_in(key_list[9], 1), 0, 1),
    }


inv_root_two = 0.7071067811865476
inv_root_tau = 0.3989422804014327

def gelu_slope(values):
    return 0.5 * (1.0 + lax.erf(values * inv_root_two)) + values * jnp.exp(-0.5 * values * values) * inv_root_tau

def halo_all(tile_field, tile_links):
    neighbour_tile, edge_code, corner_tile, corner_code, corner_missing = tile_links
    strips = jnp.stack([tile_field[:, :, 0, :], tile_field[:, :, :, -1], tile_field[:, :, -1, :], tile_field[:, :, :, 0]], axis=1)
    picked = strips[neighbour_tile, edge_code % 4]
    picked = jnp.where((edge_code >= 4)[:, :, None, None], picked[..., ::-1], picked)
    corners = jnp.stack([tile_field[:, :, 0, 0], tile_field[:, :, 0, -1], tile_field[:, :, -1, -1], tile_field[:, :, -1, 0]], axis=1)
    corner_got = corners[corner_tile, corner_code]
    corner_got = jnp.where((corner_missing == 1)[:, :, None], jnp.zeros_like(corner_got), corner_got)
    padded = jnp.pad(tile_field, ((0, 0), (0, 0), (1, 1), (1, 1)))
    padded = padded.at[:, :, 0, 1:-1].set(picked[:, 0])
    padded = padded.at[:, :, 1:-1, -1].set(picked[:, 1])
    padded = padded.at[:, :, -1, 1:-1].set(picked[:, 2])
    padded = padded.at[:, :, 1:-1, 0].set(picked[:, 3])
    padded = padded.at[:, :, 0, 0].set(corner_got[:, 0])
    padded = padded.at[:, :, 0, -1].set(corner_got[:, 1])
    padded = padded.at[:, :, -1, -1].set(corner_got[:, 2])
    padded = padded.at[:, :, -1, 0].set(corner_got[:, 3])
    return padded

def adjoint_all(back_rim, tile_links):
    dims = back_rim.shape
    zero_field = jnp.zeros((dims[0], dims[1], dims[2] - 2, dims[3] - 2), jnp.float32)

    def linear_map(values):
        return halo_all(values, tile_links)
    pulled = jax.vjp(linear_map, zero_field)[1](back_rim.astype(jnp.float32))
    return pulled[0]

def conv_cells(padded, weights):
    channels = padded.shape[0]
    cell_width = padded.shape[1] - 2
    result = jnp.zeros((weights.shape[1], cell_width * cell_width), jnp.float32)
    for tap_index in range(9):
        row_off, col_off = divmod(tap_index, 3)
        window = padded[:, row_off:row_off + cell_width, col_off:col_off + cell_width].reshape(channels, cell_width * cell_width)
        result = result + jnp.dot(weights[tap_index], window, preferred_element_type=jnp.float32)
    return result

def spread_back(grad_rows, weights, cell_width):
    grad_grid = grad_rows.reshape(grad_rows.shape[0], cell_width, cell_width)
    wide_grid = jnp.pad(grad_grid, ((0, 0), (2, 2), (2, 2)))
    ext_width = cell_width + 2
    result = jnp.zeros((weights.shape[2], ext_width * ext_width), jnp.float32)
    for tap_index in range(9):
        row_off, col_off = divmod(tap_index, 3)
        window = wide_grid[:, 2 - row_off:2 - row_off + ext_width, 2 - col_off:2 - col_off + ext_width].reshape(grad_rows.shape[0], ext_width * ext_width)
        result = result + jnp.dot(weights[tap_index].T, window, preferred_element_type=jnp.float32)
    return result.reshape(weights.shape[2], ext_width, ext_width)

def weight_terms(padded, grad_rows, cell_width):
    channels = padded.shape[0]
    term_list = []
    for tap_index in range(9):
        row_off, col_off = divmod(tap_index, 3)
        window = padded[:, row_off:row_off + cell_width, col_off:col_off + cell_width].reshape(channels, cell_width * cell_width)
        term_list.append(jnp.dot(grad_rows, window.T, preferred_element_type=jnp.float32))
    return jnp.stack(term_list, axis=0)

def reference(fields, conv_a, bias_a, conv_b, cotangent, neighbour_tile, edge_code, corner_tile, corner_code, corner_missing):
    tile_links = (neighbour_tile, edge_code, corner_tile, corner_code, corner_missing)
    channels = fields.shape[1]
    padded_x = halo_all(fields.reshape(TILES, channels, SIDE, SIDE), tile_links)

    def forward_part(padded):
        pre_act = conv_cells(padded, conv_a) + bias_a[:, None]
        return (jax.nn.gelu(pre_act, approximate=False).astype(jnp.bfloat16), pre_act.astype(jnp.bfloat16))
    activation, pre_saved = lax.map(forward_part, padded_x)
    padded_act = halo_all(activation.reshape(TILES, channels, SIDE, SIDE), tile_links)

    def second_part(operands):
        padded, field_row, upstream = operands
        output_row = (field_row.astype(jnp.float32) + conv_cells(padded, conv_b)).astype(jnp.bfloat16)
        back_rim = spread_back(upstream, conv_b, SIDE).astype(jnp.bfloat16)
        return (output_row, back_rim, weight_terms(padded, upstream, SIDE))
    output, back_act, terms_b = lax.map(second_part, (padded_act, fields, cotangent))
    grad_act = adjoint_all(back_act, tile_links)

    def third_part(operands):
        padded, saved, grad_cells = operands
        grad_pre = (grad_cells.reshape(channels, SIDE * SIDE) * gelu_slope(saved.astype(jnp.float32))).astype(jnp.bfloat16)
        back_rim = spread_back(grad_pre, conv_a, SIDE).astype(jnp.bfloat16)
        return (back_rim, weight_terms(padded, grad_pre, SIDE), lax.optimization_barrier(jnp.sum(grad_pre.astype(jnp.float32), axis=1)))
    back_x, terms_a, terms_bias = lax.map(third_part, (padded_x, pre_saved, grad_act))
    pulled_x = adjoint_all(back_x, tile_links).reshape(TILES, channels, SIDE * SIDE)
    grad_fields = (cotangent.astype(jnp.float32) + pulled_x).astype(jnp.bfloat16)
    grad_scale = (TILES * SIDE * SIDE) ** (-0.5)
    grad_a = lax.optimization_barrier(jnp.sum(terms_a, axis=0)) * grad_scale
    grad_b = lax.optimization_barrier(jnp.sum(terms_b, axis=0)) * grad_scale
    grad_bias = lax.optimization_barrier(jnp.sum(terms_bias, axis=0)) * grad_scale
    return (output, grad_fields, grad_a, grad_b, grad_bias)
```

```python
import jax
import jax.numpy as jnp
from jax import lax
from jax.sharding import PartitionSpec as P

SIDE = 16
TILE_ROW = 8


inv_root_two = 0.7071067811865476
inv_root_tau = 0.3989422804014327


def passed_along(block, axis, distance):
    devices = range(lax.axis_size(axis))
    route = [((i - distance) % len(devices), i) for i in devices]
    return lax.ppermute(block, axis, route)


def gelu_slope(values):
    return (
        0.5 * (1.0 + lax.erf(values * inv_root_two))
        + values * jnp.exp(-0.5 * values * values) * inv_root_tau
    )


def strip_sides(tile_field):
    return jnp.stack(
        [tile_field[:, 0, :], tile_field[:, :, -1], tile_field[:, -1, :], tile_field[:, :, 0]],
        axis=0,
    )


def rim_sides(padded):
    return jnp.stack(
        [padded[:, 0, 1:-1], padded[:, 1:-1, -1], padded[:, -1, 1:-1], padded[:, 1:-1, 0]], axis=0
    )


def corner_cells(tile_field):
    return jnp.stack(
        [tile_field[:, 0, 0], tile_field[:, 0, -1], tile_field[:, -1, -1], tile_field[:, -1, 0]],
        axis=0,
    )


def offset_class(linked, offsets):
    device_count = lax.axis_size("tiles")
    own_index = lax.axis_index("tiles")
    relative = (linked - own_index) % device_count
    targets = jnp.array([shift_by % device_count for shift_by in offsets], dtype=jnp.int32)
    matches = (relative[:, None] == targets[None, :]).astype(jnp.int32)
    classes = jnp.sum(matches * jnp.arange(4, dtype=jnp.int32)[None, :], axis=1)
    return (matches, classes)


def exchange_groups(strip_groups, corner_groups, tile_links):
    neighbour_ids, edge_codes, corner_ids, corner_codes = tile_links
    row_length = TILE_ROW
    edge_offsets = [-row_length, 1, row_length, -1]
    diag_offsets = [1 - row_length, 1 + row_length, row_length - 1, -1 - row_length]
    _, edge_class = offset_class(neighbour_ids, edge_offsets)
    _, diag_class = offset_class(corner_ids, diag_offsets)
    groups = len(strip_groups)
    strips = jnp.concatenate(strip_groups, axis=0)
    corners = jnp.concatenate(corner_groups, axis=0)
    received = [passed_along(strips, "tiles", -edge_offsets[d]) for d in range(4)]
    stacked = jnp.concatenate(received, axis=0)
    corner_recv = [passed_along(corners, "tiles", -diag_offsets[d]) for d in range(4)]
    corner_stack = jnp.concatenate(corner_recv, axis=0)
    reverse = (edge_codes >= 4)[:, None, None]
    their_side = edge_codes % 4
    out = []
    for g in range(groups):
        picked = stacked[edge_class * (4 * groups) + 4 * g + their_side]
        picked = jnp.where(reverse, picked[:, :, ::-1], picked)
        corner_got = corner_stack[diag_class * (4 * groups) + 4 * g + corner_codes]
        out.append((picked, corner_got))
    return out


def assemble_padded(tile_field, picked, corner_got, missing):
    corner_got = jnp.where((missing == 1)[:, None], jnp.zeros_like(corner_got), corner_got)
    top = jnp.concatenate(
        [corner_got[0][:, None], picked[0], corner_got[1][:, None]], axis=1
    )
    bottom = jnp.concatenate(
        [corner_got[3][:, None], picked[2], corner_got[2][:, None]], axis=1
    )
    middle = jnp.concatenate(
        [picked[3][:, :, None], tile_field, picked[1][:, :, None]], axis=2
    )
    return jnp.concatenate([top[:, None, :], middle, bottom[:, None, :]], axis=1)


def rim_payload(back_rim, missing):
    rim_corner = corner_cells(back_rim)
    rim_corner = jnp.where((missing == 1)[:, None], jnp.zeros_like(rim_corner), rim_corner)
    return rim_sides(back_rim), rim_corner


def adjoint_sum(back_rim, picked, corner_got):
    summed = back_rim[:, 1:-1, 1:-1].astype(jnp.float32)
    p = picked.astype(jnp.float32)
    c = corner_got.astype(jnp.float32)
    side = SIDE
    summed = summed + jnp.pad(p[0][:, None, :], ((0, 0), (0, side - 1), (0, 0)))
    summed = summed + jnp.pad(p[2][:, None, :], ((0, 0), (side - 1, 0), (0, 0)))
    summed = summed + jnp.pad(p[3][:, :, None], ((0, 0), (0, 0), (0, side - 1)))
    summed = summed + jnp.pad(p[1][:, :, None], ((0, 0), (0, 0), (side - 1, 0)))
    corner_grid = jnp.stack(
        [
            jnp.stack([c[0], c[1]], axis=-1),
            jnp.stack([c[3], c[2]], axis=-1),
        ],
        axis=-2,
    )
    full = jnp.zeros_like(summed)
    full = full.at[:, 0::side - 1, 0::side - 1].set(corner_grid)
    return summed + full


def conv_cells(padded, weights):
    channels = padded.shape[0]
    cell_width = padded.shape[1] - 2
    result = jnp.zeros((weights.shape[1], cell_width * cell_width), jnp.float32)
    for tap_index in range(9):
        row_off, col_off = divmod(tap_index, 3)
        window = padded[:, row_off : row_off + cell_width, col_off : col_off + cell_width].reshape(
            channels, cell_width * cell_width
        )
        result = result + jnp.dot(weights[tap_index], window, preferred_element_type=jnp.float32)
    return result


def spread_back(grad_rows, weights, cell_width):
    grad_grid = grad_rows.reshape(grad_rows.shape[0], cell_width, cell_width)
    wide_grid = jnp.pad(grad_grid, ((0, 0), (2, 2), (2, 2)))
    ext_width = cell_width + 2
    result = jnp.zeros((weights.shape[2], ext_width * ext_width), jnp.float32)
    for tap_index in range(9):
        row_off, col_off = divmod(tap_index, 3)
        window = wide_grid[
            :, 2 - row_off : 2 - row_off + ext_width, 2 - col_off : 2 - col_off + ext_width
        ].reshape(grad_rows.shape[0], ext_width * ext_width)
        result = result + lax.dot_general(
            weights[tap_index], window, (((0,), (0,)), ((), ())), preferred_element_type=jnp.float32
        )
    return result.reshape(weights.shape[2], ext_width, ext_width)


def weight_terms(padded, grad_rows, cell_width):
    channels = padded.shape[0]
    term_list = []
    for tap_index in range(9):
        row_off, col_off = divmod(tap_index, 3)
        window = padded[:, row_off : row_off + cell_width, col_off : col_off + cell_width].reshape(
            channels, cell_width * cell_width
        )
        term_list.append(
            lax.dot_general(
                grad_rows, window, (((1,), (1,)), ((), ())), preferred_element_type=jnp.float32
            )
        )
    return jnp.stack(term_list, axis=0)


def body(
    fields,
    conv_a,
    bias_a,
    conv_b,
    cotangent,
    neighbour_tile,
    edge_code,
    corner_tile,
    corner_code,
    corner_missing,
):
    channels = fields.shape[1]
    cell_width = SIDE
    tile_links = (neighbour_tile[0], edge_code[0], corner_tile[0], corner_code[0])
    missing = corner_missing[0]
    field_grid = fields[0].reshape(channels, cell_width, cell_width)
    upstream = cotangent[0]
    back_act = spread_back(upstream, conv_b, cell_width).astype(jnp.bfloat16)
    act_rims, act_rim_corners = rim_payload(back_act, missing)
    (x_picked, x_corners), (ba_picked, ba_corners) = exchange_groups(
        [strip_sides(field_grid), act_rims],
        [corner_cells(field_grid), act_rim_corners],
        tile_links,
    )
    padded_x = assemble_padded(field_grid, x_picked, x_corners, missing)
    pre_act = conv_cells(padded_x, conv_a) + bias_a[:, None]
    activation = jax.nn.gelu(pre_act, approximate=False).astype(jnp.bfloat16)
    pre_saved = pre_act.astype(jnp.bfloat16)
    grad_act = adjoint_sum(back_act, ba_picked, ba_corners)
    grad_pre = (
        grad_act.reshape(channels, cell_width * cell_width)
        * gelu_slope(pre_saved.astype(jnp.float32))
    ).astype(jnp.bfloat16)
    back_x = spread_back(grad_pre, conv_a, cell_width).astype(jnp.bfloat16)
    terms_a = weight_terms(padded_x, grad_pre, cell_width)
    terms_bias = jnp.sum(grad_pre, axis=1, dtype=jnp.float32)
    act_grid = activation.reshape(channels, cell_width, cell_width)
    x_rims, x_rim_corners = rim_payload(back_x, missing)
    (a_picked, a_corners), (bx_picked, bx_corners) = exchange_groups(
        [strip_sides(act_grid), x_rims],
        [corner_cells(act_grid), x_rim_corners],
        tile_links,
    )
    padded_act = assemble_padded(act_grid, a_picked, a_corners, missing)
    output = (fields[0].astype(jnp.float32) + conv_cells(padded_act, conv_b)).astype(jnp.bfloat16)
    terms_b = weight_terms(padded_act, upstream, cell_width)
    tap_size = terms_a.size
    flat = jnp.concatenate([terms_a.reshape(-1), terms_b.reshape(-1), terms_bias])
    summed = lax.psum(flat, "tiles")
    summed_a = summed[:tap_size].reshape(terms_a.shape)
    summed_b = summed[tap_size : 2 * tap_size].reshape(terms_b.shape)
    summed_bias = summed[2 * tap_size :]
    pulled_x = adjoint_sum(back_x, bx_picked, bx_corners).reshape(
        channels, cell_width * cell_width
    )
    grad_fields = (upstream.astype(jnp.float32) + pulled_x).astype(jnp.bfloat16)
    grad_scale = (lax.axis_size("tiles") * cell_width * cell_width) ** (-0.5)
    return (
        output[None],
        grad_fields[None],
        summed_a * grad_scale,
        summed_b * grad_scale,
        summed_bias * grad_scale,
    )


def solution(mesh):
    return jax.shard_map(
        body,
        mesh=mesh,
        in_specs=(
            P("tiles", None, None),
            P(),
            P(),
            P(),
            P("tiles", None, None),
            P("tiles", None),
            P("tiles", None),
            P("tiles", None),
            P("tiles", None),
            P("tiles", None),
        ),
        out_specs=(P("tiles", None, None), P("tiles", None, None), P(), P(), P()),
        check_vma=False,
    )
```

```python
import jax
import jax.numpy as jnp
from jax import lax
from jax.sharding import PartitionSpec as P

SIDE = 16
TILE_ROW = 8
HALVING_ROUNDS = 3


inv_root_two = 0.7071067811865476
inv_root_tau = 0.3989422804014327


def passed_along(block, axis, distance):
    devices = range(lax.axis_size(axis))
    route = [((i - distance) % len(devices), i) for i in devices]
    return lax.ppermute(block, axis, route)


def xor_partner(block, distance):
    devices = lax.axis_size("tiles")
    return lax.ppermute(block, "tiles", [(i, i ^ distance) for i in range(devices)])


def tree_all_reduce(flat, halving_rounds):
    devices = lax.axis_size("tiles")
    bits = devices.bit_length() - 1
    own = lax.axis_index("tiles")
    halving_rounds = min(halving_rounds, bits)
    quantum = 128 << halving_rounds
    length = flat.shape[0]
    padded = -(-length // quantum) * quantum
    cur = jnp.pad(flat, (0, padded - length))
    for k in range(halving_rounds):
        half = cur.shape[0] // 2
        upper = ((own >> k) & 1) == 1
        low, high = cur[:half], cur[half:]
        keep = jnp.where(upper, high, low)
        send = jnp.where(upper, low, high)
        cur = keep + xor_partner(send, 1 << k)
    for k in range(halving_rounds, bits):
        cur = cur + xor_partner(cur, 1 << k)
    for k in reversed(range(halving_rounds)):
        upper = ((own >> k) & 1) == 1
        got = xor_partner(cur, 1 << k)
        cur = jnp.where(upper, jnp.concatenate([got, cur]), jnp.concatenate([cur, got]))
    return cur[:length]


def gelu_slope(values):
    return (
        0.5 * (1.0 + lax.erf(values * inv_root_two))
        + values * jnp.exp(-0.5 * values * values) * inv_root_tau
    )


def strip_sides(tile_field):
    return jnp.stack(
        [tile_field[:, 0, :], tile_field[:, :, -1], tile_field[:, -1, :], tile_field[:, :, 0]],
        axis=0,
    )


def rim_sides(padded):
    return jnp.stack(
        [padded[:, 0, 1:-1], padded[:, 1:-1, -1], padded[:, -1, 1:-1], padded[:, 1:-1, 0]], axis=0
    )


def corner_cells(tile_field):
    return jnp.stack(
        [tile_field[:, 0, 0], tile_field[:, 0, -1], tile_field[:, -1, -1], tile_field[:, -1, 0]],
        axis=0,
    )


def offset_class(linked, offsets):
    device_count = lax.axis_size("tiles")
    own_index = lax.axis_index("tiles")
    relative = (linked - own_index) % device_count
    targets = jnp.array([shift_by % device_count for shift_by in offsets], dtype=jnp.int32)
    matches = (relative[:, None] == targets[None, :]).astype(jnp.int32)
    classes = jnp.sum(matches * jnp.arange(4, dtype=jnp.int32)[None, :], axis=1)
    return (matches, classes)


def exchange_groups(strip_groups, corner_groups, tile_links):
    neighbour_ids, edge_codes, corner_ids, corner_codes = tile_links
    row_length = TILE_ROW
    edge_offsets = [-row_length, 1, row_length, -1]
    diag_offsets = [1 - row_length, 1 + row_length, row_length - 1, -1 - row_length]
    _, edge_class = offset_class(neighbour_ids, edge_offsets)
    _, diag_class = offset_class(corner_ids, diag_offsets)
    groups = len(strip_groups)
    strips = jnp.concatenate(strip_groups, axis=0)
    corners = jnp.concatenate(corner_groups, axis=0)
    received = [passed_along(strips, "tiles", -edge_offsets[d]) for d in range(4)]
    stacked = jnp.concatenate(received, axis=0)
    corner_recv = [passed_along(corners, "tiles", -diag_offsets[d]) for d in range(4)]
    corner_stack = jnp.concatenate(corner_recv, axis=0)
    reverse = (edge_codes >= 4)[:, None, None]
    their_side = edge_codes % 4
    out = []
    for g in range(groups):
        picked = stacked[edge_class * (4 * groups) + 4 * g + their_side]
        picked = jnp.where(reverse, picked[:, :, ::-1], picked)
        corner_got = corner_stack[diag_class * (4 * groups) + 4 * g + corner_codes]
        out.append((picked, corner_got))
    return out


def assemble_padded(tile_field, picked, corner_got, missing):
    corner_got = jnp.where((missing == 1)[:, None], jnp.zeros_like(corner_got), corner_got)
    top = jnp.concatenate(
        [corner_got[0][:, None], picked[0], corner_got[1][:, None]], axis=1
    )
    bottom = jnp.concatenate(
        [corner_got[3][:, None], picked[2], corner_got[2][:, None]], axis=1
    )
    middle = jnp.concatenate(
        [picked[3][:, :, None], tile_field, picked[1][:, :, None]], axis=2
    )
    return jnp.concatenate([top[:, None, :], middle, bottom[:, None, :]], axis=1)


def rim_payload(back_rim, missing):
    rim_corner = corner_cells(back_rim)
    rim_corner = jnp.where((missing == 1)[:, None], jnp.zeros_like(rim_corner), rim_corner)
    return rim_sides(back_rim), rim_corner


def adjoint_sum(back_rim, picked, corner_got):
    summed = back_rim[:, 1:-1, 1:-1].astype(jnp.float32)
    p = picked.astype(jnp.float32)
    c = corner_got.astype(jnp.float32)
    side = SIDE
    summed = summed + jnp.pad(p[0][:, None, :], ((0, 0), (0, side - 1), (0, 0)))
    summed = summed + jnp.pad(p[2][:, None, :], ((0, 0), (side - 1, 0), (0, 0)))
    summed = summed + jnp.pad(p[3][:, :, None], ((0, 0), (0, 0), (0, side - 1)))
    summed = summed + jnp.pad(p[1][:, :, None], ((0, 0), (0, 0), (side - 1, 0)))
    corner_grid = jnp.stack(
        [
            jnp.stack([c[0], c[1]], axis=-1),
            jnp.stack([c[3], c[2]], axis=-1),
        ],
        axis=-2,
    )
    full = jnp.zeros_like(summed)
    full = full.at[:, 0::side - 1, 0::side - 1].set(corner_grid)
    return summed + full


def conv_cells(padded, weights):
    channels = padded.shape[0]
    cell_width = padded.shape[1] - 2
    result = jnp.zeros((weights.shape[1], cell_width * cell_width), jnp.float32)
    for tap_index in range(9):
        row_off, col_off = divmod(tap_index, 3)
        window = padded[:, row_off : row_off + cell_width, col_off : col_off + cell_width].reshape(
            channels, cell_width * cell_width
        )
        result = result + jnp.dot(weights[tap_index], window, preferred_element_type=jnp.float32)
    return result


def spread_back(grad_rows, weights, cell_width):
    grad_grid = grad_rows.reshape(grad_rows.shape[0], cell_width, cell_width)
    wide_grid = jnp.pad(grad_grid, ((0, 0), (2, 2), (2, 2)))
    ext_width = cell_width + 2
    result = jnp.zeros((weights.shape[2], ext_width * ext_width), jnp.float32)
    for tap_index in range(9):
        row_off, col_off = divmod(tap_index, 3)
        window = wide_grid[
            :, 2 - row_off : 2 - row_off + ext_width, 2 - col_off : 2 - col_off + ext_width
        ].reshape(grad_rows.shape[0], ext_width * ext_width)
        result = result + lax.dot_general(
            weights[tap_index], window, (((0,), (0,)), ((), ())), preferred_element_type=jnp.float32
        )
    return result.reshape(weights.shape[2], ext_width, ext_width)


def weight_terms(padded, grad_rows, cell_width):
    channels = padded.shape[0]
    term_list = []
    for tap_index in range(9):
        row_off, col_off = divmod(tap_index, 3)
        window = padded[:, row_off : row_off + cell_width, col_off : col_off + cell_width].reshape(
            channels, cell_width * cell_width
        )
        term_list.append(
            lax.dot_general(
                grad_rows, window, (((1,), (1,)), ((), ())), preferred_element_type=jnp.float32
            )
        )
    return jnp.stack(term_list, axis=0)


def body(
    fields,
    conv_a,
    bias_a,
    conv_b,
    cotangent,
    neighbour_tile,
    edge_code,
    corner_tile,
    corner_code,
    corner_missing,
):
    channels = fields.shape[1]
    cell_width = SIDE
    tile_links = (neighbour_tile[0], edge_code[0], corner_tile[0], corner_code[0])
    missing = corner_missing[0]
    field_grid = fields[0].reshape(channels, cell_width, cell_width)
    upstream = cotangent[0]
    back_act = spread_back(upstream, conv_b, cell_width).astype(jnp.bfloat16)
    act_rims, act_rim_corners = rim_payload(back_act, missing)
    (x_picked, x_corners), (ba_picked, ba_corners) = exchange_groups(
        [strip_sides(field_grid), act_rims],
        [corner_cells(field_grid), act_rim_corners],
        tile_links,
    )
    padded_x = assemble_padded(field_grid, x_picked, x_corners, missing)
    pre_act = conv_cells(padded_x, conv_a) + bias_a[:, None]
    activation = jax.nn.gelu(pre_act, approximate=False).astype(jnp.bfloat16)
    pre_saved = pre_act.astype(jnp.bfloat16)
    grad_act = adjoint_sum(back_act, ba_picked, ba_corners)
    grad_pre = (
        grad_act.reshape(channels, cell_width * cell_width)
        * gelu_slope(pre_saved.astype(jnp.float32))
    ).astype(jnp.bfloat16)
    back_x = spread_back(grad_pre, conv_a, cell_width).astype(jnp.bfloat16)
    terms_a = weight_terms(padded_x, grad_pre, cell_width)
    terms_bias = jnp.sum(grad_pre, axis=1, dtype=jnp.float32)
    act_grid = activation.reshape(channels, cell_width, cell_width)
    x_rims, x_rim_corners = rim_payload(back_x, missing)
    (a_picked, a_corners), (bx_picked, bx_corners) = exchange_groups(
        [strip_sides(act_grid), x_rims],
        [corner_cells(act_grid), x_rim_corners],
        tile_links,
    )
    padded_act = assemble_padded(act_grid, a_picked, a_corners, missing)
    output = (fields[0].astype(jnp.float32) + conv_cells(padded_act, conv_b)).astype(jnp.bfloat16)
    terms_b = weight_terms(padded_act, upstream, cell_width)
    tap_size = terms_a.size
    flat = jnp.concatenate([terms_a.reshape(-1), terms_b.reshape(-1), terms_bias])
    summed = tree_all_reduce(flat, HALVING_ROUNDS)
    summed_a = summed[:tap_size].reshape(terms_a.shape)
    summed_b = summed[tap_size : 2 * tap_size].reshape(terms_b.shape)
    summed_bias = summed[2 * tap_size :]
    pulled_x = adjoint_sum(back_x, bx_picked, bx_corners).reshape(
        channels, cell_width * cell_width
    )
    grad_fields = (upstream.astype(jnp.float32) + pulled_x).astype(jnp.bfloat16)
    grad_scale = (lax.axis_size("tiles") * cell_width * cell_width) ** (-0.5)
    return (
        output[None],
        grad_fields[None],
        summed_a * grad_scale,
        summed_b * grad_scale,
        summed_bias * grad_scale,
    )


def solution(mesh):
    return jax.shard_map(
        body,
        mesh=mesh,
        in_specs=(
            P("tiles", None, None),
            P(),
            P(),
            P(),
            P("tiles", None, None),
            P("tiles", None),
            P("tiles", None),
            P("tiles", None),
            P("tiles", None),
            P("tiles", None),
        ),
        out_specs=(P("tiles", None, None), P("tiles", None, None), P(), P(), P()),
        check_vma=False,
    )
```

```python
import jax
import jax.numpy as jnp
from jax import lax
from jax.sharding import PartitionSpec as P

SIDE = 16
TILE_ROW = 8
HALVING_ROUNDS = 3


inv_root_two = 0.7071067811865476
inv_root_tau = 0.3989422804014327


def passed_along(block, axis, distance):
    devices = range(lax.axis_size(axis))
    route = [((i - distance) % len(devices), i) for i in devices]
    return lax.ppermute(block, axis, route)


def xor_partner(block, distance):
    devices = lax.axis_size("tiles")
    return lax.ppermute(block, "tiles", [(i, i ^ distance) for i in range(devices)])


def tree_all_reduce(flat, halving_rounds):
    devices = lax.axis_size("tiles")
    bits = devices.bit_length() - 1
    own = lax.axis_index("tiles")
    halving_rounds = min(halving_rounds, bits)
    quantum = 128 << halving_rounds
    length = flat.shape[0]
    padded = -(-length // quantum) * quantum
    cur = jnp.pad(flat, (0, padded - length))
    for k in range(halving_rounds):
        half = cur.shape[0] // 2
        upper = ((own >> k) & 1) == 1
        low, high = cur[:half], cur[half:]
        keep = jnp.where(upper, high, low)
        send = jnp.where(upper, low, high)
        cur = keep + xor_partner(send, 1 << k)
    for k in range(halving_rounds, bits):
        cur = cur + xor_partner(cur, 1 << k)
    for k in reversed(range(halving_rounds)):
        upper = ((own >> k) & 1) == 1
        got = xor_partner(cur, 1 << k)
        cur = jnp.where(upper, jnp.concatenate([got, cur]), jnp.concatenate([cur, got]))
    return cur[:length]


def gelu_slope(values):
    return (
        0.5 * (1.0 + lax.erf(values * inv_root_two))
        + values * jnp.exp(-0.5 * values * values) * inv_root_tau
    )


def strip_sides(tile_field):
    return jnp.stack(
        [tile_field[:, 0, :], tile_field[:, :, -1], tile_field[:, -1, :], tile_field[:, :, 0]],
        axis=0,
    )


def rim_sides(padded):
    return jnp.stack(
        [padded[:, 0, 1:-1], padded[:, 1:-1, -1], padded[:, -1, 1:-1], padded[:, 1:-1, 0]], axis=0
    )


def corner_cells(tile_field):
    return jnp.stack(
        [tile_field[:, 0, 0], tile_field[:, 0, -1], tile_field[:, -1, -1], tile_field[:, -1, 0]],
        axis=0,
    )


def offset_class(linked, offsets):
    device_count = lax.axis_size("tiles")
    own_index = lax.axis_index("tiles")
    relative = (linked - own_index) % device_count
    targets = jnp.array([shift_by % device_count for shift_by in offsets], dtype=jnp.int32)
    matches = (relative[:, None] == targets[None, :]).astype(jnp.int32)
    classes = jnp.sum(matches * jnp.arange(4, dtype=jnp.int32)[None, :], axis=1)
    return (matches, classes)


def corner_row(corners, width):
    block = jnp.transpose(corners, (1, 0))
    block = jnp.pad(block, ((0, 0), (0, width - block.shape[1])))
    return block[None]


def exchange_groups(strip_groups, corner_groups, tile_links):
    neighbour_ids, edge_codes, corner_ids, corner_codes = tile_links
    row_length = TILE_ROW
    edge_offsets = [-row_length, 1, row_length, -1]
    diag_offsets = [1 - row_length, 1 + row_length, row_length - 1, -1 - row_length]
    _, edge_class = offset_class(neighbour_ids, edge_offsets)
    _, diag_class = offset_class(corner_ids, diag_offsets)
    groups = len(strip_groups)
    n_strips = 4 * groups
    strips = jnp.concatenate(strip_groups, axis=0)
    corners = jnp.concatenate(corner_groups, axis=0)
    width = strips.shape[2]
    payload_a = jnp.concatenate([strips, corner_row(corners, width)], axis=0)
    from_next = passed_along(payload_a, "tiles", -1)
    from_prev = passed_along(payload_a, "tiles", 1)
    corners_next = jnp.transpose(from_next[n_strips, :, :n_strips], (1, 0))
    corners_prev = jnp.transpose(from_prev[n_strips, :, :n_strips], (1, 0))
    relay = jnp.concatenate([corners_next, corners_prev], axis=0)
    payload_b = jnp.concatenate([strips, corner_row(relay, width)], axis=0)
    from_up = passed_along(payload_b, "tiles", row_length)
    from_down = passed_along(payload_b, "tiles", -row_length)
    stacked = jnp.concatenate(
        [from_up[:n_strips], from_next[:n_strips], from_down[:n_strips], from_prev[:n_strips]],
        axis=0,
    )
    up_relay = jnp.transpose(from_up[n_strips, :, : 2 * n_strips], (1, 0))
    down_relay = jnp.transpose(from_down[n_strips, :, : 2 * n_strips], (1, 0))
    corner_stack = jnp.concatenate(
        [up_relay[:n_strips], down_relay[:n_strips], down_relay[n_strips:], up_relay[n_strips:]],
        axis=0,
    )
    reverse = (edge_codes >= 4)[:, None, None]
    their_side = edge_codes % 4
    out = []
    for g in range(groups):
        picked = stacked[edge_class * n_strips + 4 * g + their_side]
        picked = jnp.where(reverse, picked[:, :, ::-1], picked)
        corner_got = corner_stack[diag_class * n_strips + 4 * g + corner_codes]
        out.append((picked, corner_got))
    return out


def assemble_padded(tile_field, picked, corner_got, missing):
    corner_got = jnp.where((missing == 1)[:, None], jnp.zeros_like(corner_got), corner_got)
    top = jnp.concatenate(
        [corner_got[0][:, None], picked[0], corner_got[1][:, None]], axis=1
    )
    bottom = jnp.concatenate(
        [corner_got[3][:, None], picked[2], corner_got[2][:, None]], axis=1
    )
    middle = jnp.concatenate(
        [picked[3][:, :, None], tile_field, picked[1][:, :, None]], axis=2
    )
    return jnp.concatenate([top[:, None, :], middle, bottom[:, None, :]], axis=1)


def rim_payload(back_rim, missing):
    rim_corner = corner_cells(back_rim)
    rim_corner = jnp.where((missing == 1)[:, None], jnp.zeros_like(rim_corner), rim_corner)
    return rim_sides(back_rim), rim_corner


def adjoint_sum(back_rim, picked, corner_got):
    summed = back_rim[:, 1:-1, 1:-1].astype(jnp.float32)
    p = picked.astype(jnp.float32)
    c = corner_got.astype(jnp.float32)
    side = SIDE
    summed = summed + jnp.pad(p[0][:, None, :], ((0, 0), (0, side - 1), (0, 0)))
    summed = summed + jnp.pad(p[2][:, None, :], ((0, 0), (side - 1, 0), (0, 0)))
    summed = summed + jnp.pad(p[3][:, :, None], ((0, 0), (0, 0), (0, side - 1)))
    summed = summed + jnp.pad(p[1][:, :, None], ((0, 0), (0, 0), (side - 1, 0)))
    corner_grid = jnp.stack(
        [
            jnp.stack([c[0], c[1]], axis=-1),
            jnp.stack([c[3], c[2]], axis=-1),
        ],
        axis=-2,
    )
    full = jnp.zeros_like(summed)
    full = full.at[:, 0::side - 1, 0::side - 1].set(corner_grid)
    return summed + full


def conv_cells(padded, weights):
    channels = padded.shape[0]
    cell_width = padded.shape[1] - 2
    result = jnp.zeros((weights.shape[1], cell_width * cell_width), jnp.float32)
    for tap_index in range(9):
        row_off, col_off = divmod(tap_index, 3)
        window = padded[:, row_off : row_off + cell_width, col_off : col_off + cell_width].reshape(
            channels, cell_width * cell_width
        )
        result = result + jnp.dot(weights[tap_index], window, preferred_element_type=jnp.float32)
    return result


def spread_back(grad_rows, weights, cell_width):
    grad_grid = grad_rows.reshape(grad_rows.shape[0], cell_width, cell_width)
    wide_grid = jnp.pad(grad_grid, ((0, 0), (2, 2), (2, 2)))
    ext_width = cell_width + 2
    result = jnp.zeros((weights.shape[2], ext_width * ext_width), jnp.float32)
    for tap_index in range(9):
        row_off, col_off = divmod(tap_index, 3)
        window = wide_grid[
            :, 2 - row_off : 2 - row_off + ext_width, 2 - col_off : 2 - col_off + ext_width
        ].reshape(grad_rows.shape[0], ext_width * ext_width)
        result = result + lax.dot_general(
            weights[tap_index], window, (((0,), (0,)), ((), ())), preferred_element_type=jnp.float32
        )
    return result.reshape(weights.shape[2], ext_width, ext_width)


def weight_terms(padded, grad_rows, cell_width):
    channels = padded.shape[0]
    term_list = []
    for tap_index in range(9):
        row_off, col_off = divmod(tap_index, 3)
        window = padded[:, row_off : row_off + cell_width, col_off : col_off + cell_width].reshape(
            channels, cell_width * cell_width
        )
        term_list.append(
            lax.dot_general(
                grad_rows, window, (((1,), (1,)), ((), ())), preferred_element_type=jnp.float32
            )
        )
    return jnp.stack(term_list, axis=0)


def body(
    fields,
    conv_a,
    bias_a,
    conv_b,
    cotangent,
    neighbour_tile,
    edge_code,
    corner_tile,
    corner_code,
    corner_missing,
):
    channels = fields.shape[1]
    cell_width = SIDE
    tile_links = (neighbour_tile[0], edge_code[0], corner_tile[0], corner_code[0])
    missing = corner_missing[0]
    field_grid = fields[0].reshape(channels, cell_width, cell_width)
    upstream = cotangent[0]
    back_act = spread_back(upstream, conv_b, cell_width).astype(jnp.bfloat16)
    act_rims, act_rim_corners = rim_payload(back_act, missing)
    (x_picked, x_corners), (ba_picked, ba_corners) = exchange_groups(
        [strip_sides(field_grid), act_rims],
        [corner_cells(field_grid), act_rim_corners],
        tile_links,
    )
    padded_x = assemble_padded(field_grid, x_picked, x_corners, missing)
    pre_act = conv_cells(padded_x, conv_a) + bias_a[:, None]
    activation = jax.nn.gelu(pre_act, approximate=False).astype(jnp.bfloat16)
    pre_saved = pre_act.astype(jnp.bfloat16)
    grad_act = adjoint_sum(back_act, ba_picked, ba_corners)
    grad_pre = (
        grad_act.reshape(channels, cell_width * cell_width)
        * gelu_slope(pre_saved.astype(jnp.float32))
    ).astype(jnp.bfloat16)
    back_x = spread_back(grad_pre, conv_a, cell_width).astype(jnp.bfloat16)
    terms_a = weight_terms(padded_x, grad_pre, cell_width)
    terms_bias = jnp.sum(grad_pre, axis=1, dtype=jnp.float32)
    act_grid = activation.reshape(channels, cell_width, cell_width)
    x_rims, x_rim_corners = rim_payload(back_x, missing)
    (a_picked, a_corners), (bx_picked, bx_corners) = exchange_groups(
        [strip_sides(act_grid), x_rims],
        [corner_cells(act_grid), x_rim_corners],
        tile_links,
    )
    padded_act = assemble_padded(act_grid, a_picked, a_corners, missing)
    output = (fields[0].astype(jnp.float32) + conv_cells(padded_act, conv_b)).astype(jnp.bfloat16)
    terms_b = weight_terms(padded_act, upstream, cell_width)
    tap_size = terms_a.size
    flat = jnp.concatenate([terms_a.reshape(-1), terms_b.reshape(-1), terms_bias])
    summed = tree_all_reduce(flat, HALVING_ROUNDS)
    summed_a = summed[:tap_size].reshape(terms_a.shape)
    summed_b = summed[tap_size : 2 * tap_size].reshape(terms_b.shape)
    summed_bias = summed[2 * tap_size :]
    pulled_x = adjoint_sum(back_x, bx_picked, bx_corners).reshape(
        channels, cell_width * cell_width
    )
    grad_fields = (upstream.astype(jnp.float32) + pulled_x).astype(jnp.bfloat16)
    grad_scale = (lax.axis_size("tiles") * cell_width * cell_width) ** (-0.5)
    return (
        output[None],
        grad_fields[None],
        summed_a * grad_scale,
        summed_b * grad_scale,
        summed_bias * grad_scale,
    )


def solution(mesh):
    return jax.shard_map(
        body,
        mesh=mesh,
        in_specs=(
            P("tiles", None, None),
            P(),
            P(),
            P(),
            P("tiles", None, None),
            P("tiles", None),
            P("tiles", None),
            P("tiles", None),
            P("tiles", None),
            P("tiles", None),
        ),
        out_specs=(P("tiles", None, None), P("tiles", None, None), P(), P(), P()),
        check_vma=False,
    )
```

```python
import jax
import jax.numpy as jnp
from jax import lax
from jax.sharding import PartitionSpec as P

SIDE = 16
TILE_ROW = 8
HALVING_ROUNDS = 3


inv_root_two = 0.7071067811865476
inv_root_tau = 0.3989422804014327


def passed_along(block, axis, distance):
    devices = range(lax.axis_size(axis))
    route = [((i - distance) % len(devices), i) for i in devices]
    return lax.ppermute(block, axis, route)


def xor_partner(block, distance):
    devices = lax.axis_size("tiles")
    return lax.ppermute(block, "tiles", [(i, i ^ distance) for i in range(devices)])


def tree_all_reduce(flat, halving_rounds):
    devices = lax.axis_size("tiles")
    bits = devices.bit_length() - 1
    own = lax.axis_index("tiles")
    halving_rounds = min(halving_rounds, bits)
    quantum = 128 << halving_rounds
    length = flat.shape[0]
    padded = -(-length // quantum) * quantum
    cur = jnp.pad(flat, (0, padded - length))
    for k in range(halving_rounds):
        half = cur.shape[0] // 2
        upper = ((own >> k) & 1) == 1
        low, high = cur[:half], cur[half:]
        keep = jnp.where(upper, high, low)
        send = jnp.where(upper, low, high)
        cur = keep + xor_partner(send, 1 << k)
    for k in range(halving_rounds, bits):
        cur = cur + xor_partner(cur, 1 << k)
    for k in reversed(range(halving_rounds)):
        upper = ((own >> k) & 1) == 1
        got = xor_partner(cur, 1 << k)
        cur = jnp.where(upper, jnp.concatenate([got, cur]), jnp.concatenate([cur, got]))
    return cur[:length]


def gelu_slope(values):
    return (
        0.5 * (1.0 + lax.erf(values * inv_root_two))
        + values * jnp.exp(-0.5 * values * values) * inv_root_tau
    )


def strip_sides(tile_field):
    return jnp.stack(
        [tile_field[:, 0, :], tile_field[:, :, -1], tile_field[:, -1, :], tile_field[:, :, 0]],
        axis=0,
    )


def rim_sides(padded):
    return jnp.stack(
        [padded[:, 0, 1:-1], padded[:, 1:-1, -1], padded[:, -1, 1:-1], padded[:, 1:-1, 0]], axis=0
    )


def corner_cells(tile_field):
    return jnp.stack(
        [tile_field[:, 0, 0], tile_field[:, 0, -1], tile_field[:, -1, -1], tile_field[:, -1, 0]],
        axis=0,
    )


def offset_class(linked, offsets):
    device_count = lax.axis_size("tiles")
    own_index = lax.axis_index("tiles")
    relative = (linked - own_index) % device_count
    targets = jnp.array([shift_by % device_count for shift_by in offsets], dtype=jnp.int32)
    matches = (relative[:, None] == targets[None, :]).astype(jnp.int32)
    classes = jnp.sum(matches * jnp.arange(4, dtype=jnp.int32)[None, :], axis=1)
    return (matches, classes)


def corner_row(corners, width):
    block = jnp.transpose(corners, (1, 0))
    block = jnp.pad(block, ((0, 0), (0, width - block.shape[1])))
    return block[None]


def exchange_groups(strip_groups, corner_groups, tile_links):
    neighbour_ids, edge_codes, corner_ids, corner_codes = tile_links
    row_length = TILE_ROW
    edge_offsets = [-row_length, 1, row_length, -1]
    diag_offsets = [1 - row_length, 1 + row_length, row_length - 1, -1 - row_length]
    _, edge_class = offset_class(neighbour_ids, edge_offsets)
    _, diag_class = offset_class(corner_ids, diag_offsets)
    groups = len(strip_groups)
    n_strips = 4 * groups
    strips = jnp.concatenate(strip_groups, axis=0)
    corners = jnp.concatenate(corner_groups, axis=0)
    width = strips.shape[2]
    payload_a = jnp.concatenate([strips, corner_row(corners, width)], axis=0)
    from_next = passed_along(payload_a, "tiles", -1)
    from_prev = passed_along(payload_a, "tiles", 1)
    corners_next = jnp.transpose(from_next[n_strips, :, :n_strips], (1, 0))
    corners_prev = jnp.transpose(from_prev[n_strips, :, :n_strips], (1, 0))
    relay = jnp.concatenate([corners_next, corners_prev], axis=0)
    payload_b = jnp.concatenate([strips, corner_row(relay, width)], axis=0)
    from_up = passed_along(payload_b, "tiles", row_length)
    from_down = passed_along(payload_b, "tiles", -row_length)
    stacked = jnp.concatenate(
        [from_up[:n_strips], from_next[:n_strips], from_down[:n_strips], from_prev[:n_strips]],
        axis=0,
    )
    up_relay = jnp.transpose(from_up[n_strips, :, : 2 * n_strips], (1, 0))
    down_relay = jnp.transpose(from_down[n_strips, :, : 2 * n_strips], (1, 0))
    corner_stack = jnp.concatenate(
        [up_relay[:n_strips], down_relay[:n_strips], down_relay[n_strips:], up_relay[n_strips:]],
        axis=0,
    )
    reverse = (edge_codes >= 4)[:, None, None]
    their_side = edge_codes % 4
    out = []
    for g in range(groups):
        picked = stacked[edge_class * n_strips + 4 * g + their_side]
        picked = jnp.where(reverse, picked[:, :, ::-1], picked)
        corner_got = corner_stack[diag_class * n_strips + 4 * g + corner_codes]
        out.append((picked, corner_got))
    return out


def assemble_padded(tile_field, picked, corner_got, missing):
    corner_got = jnp.where((missing == 1)[:, None], jnp.zeros_like(corner_got), corner_got)
    top = jnp.concatenate(
        [corner_got[0][:, None], picked[0], corner_got[1][:, None]], axis=1
    )
    bottom = jnp.concatenate(
        [corner_got[3][:, None], picked[2], corner_got[2][:, None]], axis=1
    )
    middle = jnp.concatenate(
        [picked[3][:, :, None], tile_field, picked[1][:, :, None]], axis=2
    )
    return jnp.concatenate([top[:, None, :], middle, bottom[:, None, :]], axis=1)


def rim_payload(back_rim, missing):
    rim_corner = corner_cells(back_rim)
    rim_corner = jnp.where((missing == 1)[:, None], jnp.zeros_like(rim_corner), rim_corner)
    return rim_sides(back_rim), rim_corner


def adjoint_sum(back_rim, picked, corner_got):
    summed = back_rim[:, 1:-1, 1:-1].astype(jnp.float32)
    p = picked.astype(jnp.float32)
    c = corner_got.astype(jnp.float32)
    side = SIDE
    summed = summed + jnp.pad(p[0][:, None, :], ((0, 0), (0, side - 1), (0, 0)))
    summed = summed + jnp.pad(p[2][:, None, :], ((0, 0), (side - 1, 0), (0, 0)))
    summed = summed + jnp.pad(p[3][:, :, None], ((0, 0), (0, 0), (0, side - 1)))
    summed = summed + jnp.pad(p[1][:, :, None], ((0, 0), (0, 0), (side - 1, 0)))
    corner_grid = jnp.stack(
        [
            jnp.stack([c[0], c[1]], axis=-1),
            jnp.stack([c[3], c[2]], axis=-1),
        ],
        axis=-2,
    )
    full = jnp.zeros_like(summed)
    full = full.at[:, 0::side - 1, 0::side - 1].set(corner_grid)
    return summed + full


def conv_cells(padded, weights):
    channels = padded.shape[0]
    cell_width = padded.shape[1] - 2
    result = jnp.zeros((weights.shape[1], cell_width * cell_width), jnp.float32)
    for tap_index in range(9):
        row_off, col_off = divmod(tap_index, 3)
        window = padded[:, row_off : row_off + cell_width, col_off : col_off + cell_width].reshape(
            channels, cell_width * cell_width
        )
        result = result + jnp.dot(weights[tap_index], window, preferred_element_type=jnp.float32)
    return result


def spread_back(grad_rows, weights, cell_width):
    grad_grid = grad_rows.reshape(grad_rows.shape[0], cell_width, cell_width)
    wide_grid = jnp.pad(grad_grid, ((0, 0), (2, 2), (2, 2)))
    ext_width = cell_width + 2
    result = jnp.zeros((weights.shape[2], ext_width * ext_width), jnp.float32)
    for tap_index in range(9):
        row_off, col_off = divmod(tap_index, 3)
        window = wide_grid[
            :, 2 - row_off : 2 - row_off + ext_width, 2 - col_off : 2 - col_off + ext_width
        ].reshape(grad_rows.shape[0], ext_width * ext_width)
        result = result + lax.dot_general(
            weights[tap_index], window, (((0,), (0,)), ((), ())), preferred_element_type=jnp.float32
        )
    return result.reshape(weights.shape[2], ext_width, ext_width)


def weight_terms(padded, grad_rows, cell_width):
    channels = padded.shape[0]
    term_list = []
    for tap_index in range(9):
        row_off, col_off = divmod(tap_index, 3)
        window = padded[:, row_off : row_off + cell_width, col_off : col_off + cell_width].reshape(
            channels, cell_width * cell_width
        )
        term_list.append(
            lax.dot_general(
                grad_rows, window, (((1,), (1,)), ((), ())), preferred_element_type=jnp.float32
            )
        )
    return jnp.stack(term_list, axis=0)


def body(
    fields,
    conv_a,
    bias_a,
    conv_b,
    cotangent,
    neighbour_tile,
    edge_code,
    corner_tile,
    corner_code,
    corner_missing,
):
    channels = fields.shape[1]
    cell_width = SIDE
    tile_links = (neighbour_tile[0], edge_code[0], corner_tile[0], corner_code[0])
    missing = corner_missing[0]
    field_grid = fields[0].reshape(channels, cell_width, cell_width)
    upstream = cotangent[0]
    back_act = spread_back(upstream, conv_b, cell_width).astype(jnp.bfloat16)
    act_rims, act_rim_corners = rim_payload(back_act, missing)
    (x_picked, x_corners), (ba_picked, ba_corners) = exchange_groups(
        [strip_sides(field_grid), act_rims],
        [corner_cells(field_grid), act_rim_corners],
        tile_links,
    )
    padded_x = assemble_padded(field_grid, x_picked, x_corners, missing)
    pre_act = conv_cells(padded_x, conv_a) + bias_a[:, None]
    activation = jax.nn.gelu(pre_act, approximate=False).astype(jnp.bfloat16)
    pre_saved = pre_act.astype(jnp.bfloat16)
    grad_act = adjoint_sum(back_act, ba_picked, ba_corners)
    grad_pre = (
        grad_act.reshape(channels, cell_width * cell_width)
        * gelu_slope(pre_saved.astype(jnp.float32))
    ).astype(jnp.bfloat16)
    back_x = spread_back(grad_pre, conv_a, cell_width).astype(jnp.bfloat16)
    terms_a = weight_terms(padded_x, grad_pre, cell_width)
    terms_bias = jnp.sum(grad_pre, axis=1, dtype=jnp.float32)
    act_grid = activation.reshape(channels, cell_width, cell_width)
    x_rims, x_rim_corners = rim_payload(back_x, missing)
    (a_picked, a_corners), (bx_picked, bx_corners) = exchange_groups(
        [strip_sides(act_grid), x_rims],
        [corner_cells(act_grid), x_rim_corners],
        tile_links,
    )
    padded_act = assemble_padded(act_grid, a_picked, a_corners, missing)
    output = (fields[0].astype(jnp.float32) + conv_cells(padded_act, conv_b)).astype(jnp.bfloat16)
    terms_b = weight_terms(padded_act, upstream, cell_width)
    summed_ab = tree_all_reduce(
        jnp.concatenate([terms_a.reshape(-1), terms_bias]), HALVING_ROUNDS
    )
    summed_a = summed_ab[: terms_a.size].reshape(terms_a.shape)
    summed_bias = summed_ab[terms_a.size :]
    summed_b = tree_all_reduce(terms_b.reshape(-1), HALVING_ROUNDS).reshape(terms_b.shape)
    pulled_x = adjoint_sum(back_x, bx_picked, bx_corners).reshape(
        channels, cell_width * cell_width
    )
    grad_fields = (upstream.astype(jnp.float32) + pulled_x).astype(jnp.bfloat16)
    grad_scale = (lax.axis_size("tiles") * cell_width * cell_width) ** (-0.5)
    return (
        output[None],
        grad_fields[None],
        summed_a * grad_scale,
        summed_b * grad_scale,
        summed_bias * grad_scale,
    )


def solution(mesh):
    return jax.shard_map(
        body,
        mesh=mesh,
        in_specs=(
            P("tiles", None, None),
            P(),
            P(),
            P(),
            P("tiles", None, None),
            P("tiles", None),
            P("tiles", None),
            P("tiles", None),
            P("tiles", None),
            P("tiles", None),
        ),
        out_specs=(P("tiles", None, None), P("tiles", None, None), P(), P(), P()),
        check_vma=False,
    )
```

```python
import jax
import jax.numpy as jnp
from jax import lax
from jax.sharding import PartitionSpec as P

SIDE = 16
TILE_ROW = 8
HALVING_ROUNDS = 3


inv_root_two = 0.7071067811865476
inv_root_tau = 0.3989422804014327


def passed_along(block, axis, distance):
    devices = range(lax.axis_size(axis))
    route = [((i - distance) % len(devices), i) for i in devices]
    return lax.ppermute(block, axis, route)


def xor_partner(block, distance):
    devices = lax.axis_size("tiles")
    return lax.ppermute(block, "tiles", [(i, i ^ distance) for i in range(devices)])


def tree_all_reduce(flat, halving_rounds):
    devices = lax.axis_size("tiles")
    bits = devices.bit_length() - 1
    own = lax.axis_index("tiles")
    halving_rounds = min(halving_rounds, bits)
    quantum = 128 << halving_rounds
    length = flat.shape[0]
    padded = -(-length // quantum) * quantum
    cur = jnp.pad(flat, (0, padded - length))
    for k in range(halving_rounds):
        half = cur.shape[0] // 2
        upper = ((own >> k) & 1) == 1
        low, high = cur[:half], cur[half:]
        keep = jnp.where(upper, high, low)
        send = jnp.where(upper, low, high)
        cur = keep + xor_partner(send, 1 << k)
    for k in range(halving_rounds, bits):
        cur = cur + xor_partner(cur, 1 << k)
    for k in reversed(range(halving_rounds)):
        upper = ((own >> k) & 1) == 1
        got = xor_partner(cur, 1 << k)
        cur = jnp.where(upper, jnp.concatenate([got, cur]), jnp.concatenate([cur, got]))
    return cur[:length]


def paired_shift(block, distance):
    devices = lax.axis_size("tiles")
    own = lax.axis_index("tiles")
    flip = [(i, i ^ distance) for i in range(devices)]
    other = [
        (i, (i + distance) % devices if i & distance else (i - distance) % devices)
        for i in range(devices)
    ]
    got_flip = lax.ppermute(block, "tiles", flip)
    got_other = lax.ppermute(block, "tiles", other)
    low = (own & distance) == 0
    return jnp.where(low, got_flip, got_other), jnp.where(low, got_other, got_flip)


def gelu_slope(values):
    return (
        0.5 * (1.0 + lax.erf(values * inv_root_two))
        + values * jnp.exp(-0.5 * values * values) * inv_root_tau
    )


def strip_sides(tile_field):
    return jnp.stack(
        [tile_field[:, 0, :], tile_field[:, :, -1], tile_field[:, -1, :], tile_field[:, :, 0]],
        axis=0,
    )


def rim_sides(padded):
    return jnp.stack(
        [padded[:, 0, 1:-1], padded[:, 1:-1, -1], padded[:, -1, 1:-1], padded[:, 1:-1, 0]], axis=0
    )


def corner_cells(tile_field):
    return jnp.stack(
        [tile_field[:, 0, 0], tile_field[:, 0, -1], tile_field[:, -1, -1], tile_field[:, -1, 0]],
        axis=0,
    )


def offset_class(linked, offsets):
    device_count = lax.axis_size("tiles")
    own_index = lax.axis_index("tiles")
    relative = (linked - own_index) % device_count
    targets = jnp.array([shift_by % device_count for shift_by in offsets], dtype=jnp.int32)
    matches = (relative[:, None] == targets[None, :]).astype(jnp.int32)
    classes = jnp.sum(matches * jnp.arange(4, dtype=jnp.int32)[None, :], axis=1)
    return (matches, classes)


def corner_row(corners, width):
    block = jnp.transpose(corners, (1, 0))
    block = jnp.pad(block, ((0, 0), (0, width - block.shape[1])))
    return block[None]


def exchange_groups(strip_groups, corner_groups, tile_links):
    neighbour_ids, edge_codes, corner_ids, corner_codes = tile_links
    row_length = TILE_ROW
    edge_offsets = [-row_length, 1, row_length, -1]
    diag_offsets = [1 - row_length, 1 + row_length, row_length - 1, -1 - row_length]
    _, edge_class = offset_class(neighbour_ids, edge_offsets)
    _, diag_class = offset_class(corner_ids, diag_offsets)
    groups = len(strip_groups)
    n_strips = 4 * groups
    strips = jnp.concatenate(strip_groups, axis=0)
    corners = jnp.concatenate(corner_groups, axis=0)
    width = strips.shape[2]
    payload_a = jnp.concatenate([strips, corner_row(corners, width)], axis=0)
    from_next, from_prev = paired_shift(payload_a, 1)
    corners_next = jnp.transpose(from_next[n_strips, :, :n_strips], (1, 0))
    corners_prev = jnp.transpose(from_prev[n_strips, :, :n_strips], (1, 0))
    relay = jnp.concatenate([corners_next, corners_prev], axis=0)
    payload_b = jnp.concatenate([strips, corner_row(relay, width)], axis=0)
    from_down, from_up = paired_shift(payload_b, row_length)
    stacked = jnp.concatenate(
        [from_up[:n_strips], from_next[:n_strips], from_down[:n_strips], from_prev[:n_strips]],
        axis=0,
    )
    up_relay = jnp.transpose(from_up[n_strips, :, : 2 * n_strips], (1, 0))
    down_relay = jnp.transpose(from_down[n_strips, :, : 2 * n_strips], (1, 0))
    corner_stack = jnp.concatenate(
        [up_relay[:n_strips], down_relay[:n_strips], down_relay[n_strips:], up_relay[n_strips:]],
        axis=0,
    )
    reverse = (edge_codes >= 4)[:, None, None]
    their_side = edge_codes % 4
    out = []
    for g in range(groups):
        picked = stacked[edge_class * n_strips + 4 * g + their_side]
        picked = jnp.where(reverse, picked[:, :, ::-1], picked)
        corner_got = corner_stack[diag_class * n_strips + 4 * g + corner_codes]
        out.append((picked, corner_got))
    return out


def assemble_padded(tile_field, picked, corner_got, missing):
    corner_got = jnp.where((missing == 1)[:, None], jnp.zeros_like(corner_got), corner_got)
    top = jnp.concatenate(
        [corner_got[0][:, None], picked[0], corner_got[1][:, None]], axis=1
    )
    bottom = jnp.concatenate(
        [corner_got[3][:, None], picked[2], corner_got[2][:, None]], axis=1
    )
    middle = jnp.concatenate(
        [picked[3][:, :, None], tile_field, picked[1][:, :, None]], axis=2
    )
    return jnp.concatenate([top[:, None, :], middle, bottom[:, None, :]], axis=1)


def rim_payload(back_rim, missing):
    rim_corner = corner_cells(back_rim)
    rim_corner = jnp.where((missing == 1)[:, None], jnp.zeros_like(rim_corner), rim_corner)
    return rim_sides(back_rim), rim_corner


def adjoint_sum(back_rim, picked, corner_got):
    summed = back_rim[:, 1:-1, 1:-1].astype(jnp.float32)
    p = picked.astype(jnp.float32)
    c = corner_got.astype(jnp.float32)
    side = SIDE
    summed = summed + jnp.pad(p[0][:, None, :], ((0, 0), (0, side - 1), (0, 0)))
    summed = summed + jnp.pad(p[2][:, None, :], ((0, 0), (side - 1, 0), (0, 0)))
    summed = summed + jnp.pad(p[3][:, :, None], ((0, 0), (0, 0), (0, side - 1)))
    summed = summed + jnp.pad(p[1][:, :, None], ((0, 0), (0, 0), (side - 1, 0)))
    corner_grid = jnp.stack(
        [
            jnp.stack([c[0], c[1]], axis=-1),
            jnp.stack([c[3], c[2]], axis=-1),
        ],
        axis=-2,
    )
    full = jnp.zeros_like(summed)
    full = full.at[:, 0::side - 1, 0::side - 1].set(corner_grid)
    return summed + full


def conv_cells(padded, weights):
    channels = padded.shape[0]
    cell_width = padded.shape[1] - 2
    result = jnp.zeros((weights.shape[1], cell_width * cell_width), jnp.float32)
    for tap_index in range(9):
        row_off, col_off = divmod(tap_index, 3)
        window = padded[:, row_off : row_off + cell_width, col_off : col_off + cell_width].reshape(
            channels, cell_width * cell_width
        )
        result = result + jnp.dot(weights[tap_index], window, preferred_element_type=jnp.float32)
    return result


def spread_back(grad_rows, weights, cell_width):
    grad_grid = grad_rows.reshape(grad_rows.shape[0], cell_width, cell_width)
    wide_grid = jnp.pad(grad_grid, ((0, 0), (2, 2), (2, 2)))
    ext_width = cell_width + 2
    result = jnp.zeros((weights.shape[2], ext_width * ext_width), jnp.float32)
    for tap_index in range(9):
        row_off, col_off = divmod(tap_index, 3)
        window = wide_grid[
            :, 2 - row_off : 2 - row_off + ext_width, 2 - col_off : 2 - col_off + ext_width
        ].reshape(grad_rows.shape[0], ext_width * ext_width)
        result = result + lax.dot_general(
            weights[tap_index], window, (((0,), (0,)), ((), ())), preferred_element_type=jnp.float32
        )
    return result.reshape(weights.shape[2], ext_width, ext_width)


def weight_terms(padded, grad_rows, cell_width):
    channels = padded.shape[0]
    term_list = []
    for tap_index in range(9):
        row_off, col_off = divmod(tap_index, 3)
        window = padded[:, row_off : row_off + cell_width, col_off : col_off + cell_width].reshape(
            channels, cell_width * cell_width
        )
        term_list.append(
            lax.dot_general(
                grad_rows, window, (((1,), (1,)), ((), ())), preferred_element_type=jnp.float32
            )
        )
    return jnp.stack(term_list, axis=0)


def body(
    fields,
    conv_a,
    bias_a,
    conv_b,
    cotangent,
    neighbour_tile,
    edge_code,
    corner_tile,
    corner_code,
    corner_missing,
):
    channels = fields.shape[1]
    cell_width = SIDE
    tile_links = (neighbour_tile[0], edge_code[0], corner_tile[0], corner_code[0])
    missing = corner_missing[0]
    field_grid = fields[0].reshape(channels, cell_width, cell_width)
    upstream = cotangent[0]
    back_act = spread_back(upstream, conv_b, cell_width).astype(jnp.bfloat16)
    act_rims, act_rim_corners = rim_payload(back_act, missing)
    (x_picked, x_corners), (ba_picked, ba_corners) = exchange_groups(
        [strip_sides(field_grid), act_rims],
        [corner_cells(field_grid), act_rim_corners],
        tile_links,
    )
    padded_x = assemble_padded(field_grid, x_picked, x_corners, missing)
    pre_act = conv_cells(padded_x, conv_a) + bias_a[:, None]
    activation = jax.nn.gelu(pre_act, approximate=False).astype(jnp.bfloat16)
    pre_saved = pre_act.astype(jnp.bfloat16)
    grad_act = adjoint_sum(back_act, ba_picked, ba_corners)
    grad_pre = (
        grad_act.reshape(channels, cell_width * cell_width)
        * gelu_slope(pre_saved.astype(jnp.float32))
    ).astype(jnp.bfloat16)
    back_x = spread_back(grad_pre, conv_a, cell_width).astype(jnp.bfloat16)
    terms_a = weight_terms(padded_x, grad_pre, cell_width)
    terms_bias = jnp.sum(grad_pre, axis=1, dtype=jnp.float32)
    act_grid = activation.reshape(channels, cell_width, cell_width)
    x_rims, x_rim_corners = rim_payload(back_x, missing)
    (a_picked, a_corners), (bx_picked, bx_corners) = exchange_groups(
        [strip_sides(act_grid), x_rims],
        [corner_cells(act_grid), x_rim_corners],
        tile_links,
    )
    padded_act = assemble_padded(act_grid, a_picked, a_corners, missing)
    output = (fields[0].astype(jnp.float32) + conv_cells(padded_act, conv_b)).astype(jnp.bfloat16)
    terms_b = weight_terms(padded_act, upstream, cell_width)
    tap_size = terms_a.size
    flat = jnp.concatenate([terms_a.reshape(-1), terms_b.reshape(-1), terms_bias])
    summed = tree_all_reduce(flat, HALVING_ROUNDS)
    summed_a = summed[:tap_size].reshape(terms_a.shape)
    summed_b = summed[tap_size : 2 * tap_size].reshape(terms_b.shape)
    summed_bias = summed[2 * tap_size :]
    pulled_x = adjoint_sum(back_x, bx_picked, bx_corners).reshape(
        channels, cell_width * cell_width
    )
    grad_fields = (upstream.astype(jnp.float32) + pulled_x).astype(jnp.bfloat16)
    grad_scale = (lax.axis_size("tiles") * cell_width * cell_width) ** (-0.5)
    return (
        output[None],
        grad_fields[None],
        summed_a * grad_scale,
        summed_b * grad_scale,
        summed_bias * grad_scale,
    )


def solution(mesh):
    return jax.shard_map(
        body,
        mesh=mesh,
        in_specs=(
            P("tiles", None, None),
            P(),
            P(),
            P(),
            P("tiles", None, None),
            P("tiles", None),
            P("tiles", None),
            P("tiles", None),
            P("tiles", None),
            P("tiles", None),
        ),
        out_specs=(P("tiles", None, None), P("tiles", None, None), P(), P(), P()),
        check_vma=False,
    )
```

```python
import jax
import jax.numpy as jnp
from jax import lax
from jax.sharding import PartitionSpec as P

SIDE = 16
TILE_ROW = 8
HALVING_ROUNDS = 3


inv_root_two = 0.7071067811865476
inv_root_tau = 0.3989422804014327


def passed_along(block, axis, distance):
    devices = range(lax.axis_size(axis))
    route = [((i - distance) % len(devices), i) for i in devices]
    return lax.ppermute(block, axis, route)


def xor_partner(block, distance):
    devices = lax.axis_size("tiles")
    return lax.ppermute(block, "tiles", [(i, i ^ distance) for i in range(devices)])


def tree_all_reduce(flat, halving_rounds):
    devices = lax.axis_size("tiles")
    bits = devices.bit_length() - 1
    own = lax.axis_index("tiles")
    halving_rounds = min(halving_rounds, bits)
    quantum = 128 << halving_rounds
    length = flat.shape[0]
    padded = -(-length // quantum) * quantum
    cur = jnp.pad(flat, (0, padded - length))
    for k in range(halving_rounds):
        half = cur.shape[0] // 2
        upper = ((own >> k) & 1) == 1
        low, high = cur[:half], cur[half:]
        keep = jnp.where(upper, high, low)
        send = jnp.where(upper, low, high)
        cur = keep + xor_partner(send, 1 << k)
    for k in range(halving_rounds, bits):
        cur = cur + xor_partner(cur, 1 << k)
    for k in reversed(range(halving_rounds)):
        upper = ((own >> k) & 1) == 1
        got = xor_partner(cur, 1 << k)
        cur = jnp.where(upper, jnp.concatenate([got, cur]), jnp.concatenate([cur, got]))
    return cur[:length]


def paired_shift(block, distance):
    devices = lax.axis_size("tiles")
    own = lax.axis_index("tiles")
    flip = [(i, i ^ distance) for i in range(devices)]
    other = [
        (i, (i + distance) % devices if i & distance else (i - distance) % devices)
        for i in range(devices)
    ]
    got_flip = lax.ppermute(block, "tiles", flip)
    got_other = lax.ppermute(block, "tiles", other)
    low = (own & distance) == 0
    return jnp.where(low, got_flip, got_other), jnp.where(low, got_other, got_flip)


def gelu_slope(values):
    return (
        0.5 * (1.0 + lax.erf(values * inv_root_two))
        + values * jnp.exp(-0.5 * values * values) * inv_root_tau
    )


def strip_sides(tile_field):
    return jnp.stack(
        [tile_field[:, 0, :], tile_field[:, :, -1], tile_field[:, -1, :], tile_field[:, :, 0]],
        axis=0,
    )


def rim_sides(padded):
    return jnp.stack(
        [padded[:, 0, 1:-1], padded[:, 1:-1, -1], padded[:, -1, 1:-1], padded[:, 1:-1, 0]], axis=0
    )


def corner_cells(tile_field):
    return jnp.stack(
        [tile_field[:, 0, 0], tile_field[:, 0, -1], tile_field[:, -1, -1], tile_field[:, -1, 0]],
        axis=0,
    )


def offset_class(linked, offsets):
    device_count = lax.axis_size("tiles")
    own_index = lax.axis_index("tiles")
    relative = (linked - own_index) % device_count
    targets = jnp.array([shift_by % device_count for shift_by in offsets], dtype=jnp.int32)
    matches = (relative[:, None] == targets[None, :]).astype(jnp.int32)
    classes = jnp.sum(matches * jnp.arange(4, dtype=jnp.int32)[None, :], axis=1)
    return (matches, classes)


def corner_row(corners, width):
    block = jnp.transpose(corners, (1, 0))
    block = jnp.pad(block, ((0, 0), (0, width - block.shape[1])))
    return block[None]


def exchange_groups(strip_groups, corner_groups, tile_links):
    neighbour_ids, edge_codes, corner_ids, corner_codes = tile_links
    row_length = TILE_ROW
    edge_offsets = [-row_length, 1, row_length, -1]
    diag_offsets = [1 - row_length, 1 + row_length, row_length - 1, -1 - row_length]
    _, edge_class = offset_class(neighbour_ids, edge_offsets)
    _, diag_class = offset_class(corner_ids, diag_offsets)
    groups = len(strip_groups)
    n_strips = 4 * groups
    strips = jnp.concatenate(strip_groups, axis=0)
    corners = jnp.concatenate(corner_groups, axis=0)
    width = strips.shape[2]
    payload_a = jnp.concatenate([strips, corner_row(corners, width)], axis=0)
    from_next, from_prev = paired_shift(payload_a, 1)
    corners_next = jnp.transpose(from_next[n_strips, :, :n_strips], (1, 0))
    corners_prev = jnp.transpose(from_prev[n_strips, :, :n_strips], (1, 0))
    relay = jnp.concatenate([corners_next, corners_prev], axis=0)
    payload_b = jnp.concatenate([strips, corner_row(relay, width)], axis=0)
    from_down, from_up = paired_shift(payload_b, row_length)
    stacked = jnp.concatenate(
        [from_up[:n_strips], from_next[:n_strips], from_down[:n_strips], from_prev[:n_strips]],
        axis=0,
    )
    up_relay = jnp.transpose(from_up[n_strips, :, : 2 * n_strips], (1, 0))
    down_relay = jnp.transpose(from_down[n_strips, :, : 2 * n_strips], (1, 0))
    corner_stack = jnp.concatenate(
        [up_relay[:n_strips], down_relay[:n_strips], down_relay[n_strips:], up_relay[n_strips:]],
        axis=0,
    )
    reverse = (edge_codes >= 4)[:, None, None]
    their_side = edge_codes % 4
    group_ids = jnp.arange(groups, dtype=jnp.int32)[:, None] * 4
    strip_index = (edge_class * n_strips + their_side)[None, :] + group_ids
    corner_index = (diag_class * n_strips + corner_codes)[None, :] + group_ids
    picked_all = stacked[strip_index.reshape(-1)].reshape((groups, 4) + stacked.shape[1:])
    picked_all = jnp.where(reverse[None], picked_all[..., ::-1], picked_all)
    corner_all = corner_stack[corner_index.reshape(-1)].reshape(
        (groups, 4) + corner_stack.shape[1:]
    )
    return [(picked_all[g], corner_all[g]) for g in range(groups)]


def assemble_padded(tile_field, picked, corner_got, missing):
    corner_got = jnp.where((missing == 1)[:, None], jnp.zeros_like(corner_got), corner_got)
    top = jnp.concatenate(
        [corner_got[0][:, None], picked[0], corner_got[1][:, None]], axis=1
    )
    bottom = jnp.concatenate(
        [corner_got[3][:, None], picked[2], corner_got[2][:, None]], axis=1
    )
    middle = jnp.concatenate(
        [picked[3][:, :, None], tile_field, picked[1][:, :, None]], axis=2
    )
    return jnp.concatenate([top[:, None, :], middle, bottom[:, None, :]], axis=1)


def rim_payload(back_rim, missing):
    rim_corner = corner_cells(back_rim)
    rim_corner = jnp.where((missing == 1)[:, None], jnp.zeros_like(rim_corner), rim_corner)
    return rim_sides(back_rim), rim_corner


def adjoint_sum(back_rim, picked, corner_got):
    summed = back_rim[:, 1:-1, 1:-1].astype(jnp.float32)
    p = picked.astype(jnp.float32)
    c = corner_got.astype(jnp.float32)
    side = SIDE
    summed = summed + jnp.pad(p[0][:, None, :], ((0, 0), (0, side - 1), (0, 0)))
    summed = summed + jnp.pad(p[2][:, None, :], ((0, 0), (side - 1, 0), (0, 0)))
    summed = summed + jnp.pad(p[3][:, :, None], ((0, 0), (0, 0), (0, side - 1)))
    summed = summed + jnp.pad(p[1][:, :, None], ((0, 0), (0, 0), (side - 1, 0)))
    corner_grid = jnp.stack(
        [
            jnp.stack([c[0], c[1]], axis=-1),
            jnp.stack([c[3], c[2]], axis=-1),
        ],
        axis=-2,
    )
    full = lax.pad(corner_grid, jnp.float32(0), ((0, 0, 0), (0, 0, side - 2), (0, 0, side - 2)))
    return summed + full


def conv_cells(padded, weights):
    channels = padded.shape[0]
    cell_width = padded.shape[1] - 2
    result = jnp.zeros((weights.shape[1], cell_width * cell_width), jnp.float32)
    for tap_index in range(9):
        row_off, col_off = divmod(tap_index, 3)
        window = padded[:, row_off : row_off + cell_width, col_off : col_off + cell_width].reshape(
            channels, cell_width * cell_width
        )
        result = result + jnp.dot(weights[tap_index], window, preferred_element_type=jnp.float32)
    return result


def spread_back(grad_rows, weights, cell_width):
    grad_grid = grad_rows.reshape(grad_rows.shape[0], cell_width, cell_width)
    wide_grid = jnp.pad(grad_grid, ((0, 0), (2, 2), (2, 2)))
    ext_width = cell_width + 2
    result = jnp.zeros((weights.shape[2], ext_width * ext_width), jnp.float32)
    for tap_index in range(9):
        row_off, col_off = divmod(tap_index, 3)
        window = wide_grid[
            :, 2 - row_off : 2 - row_off + ext_width, 2 - col_off : 2 - col_off + ext_width
        ].reshape(grad_rows.shape[0], ext_width * ext_width)
        result = result + lax.dot_general(
            weights[tap_index], window, (((0,), (0,)), ((), ())), preferred_element_type=jnp.float32
        )
    return result.reshape(weights.shape[2], ext_width, ext_width)


def weight_terms(padded, grad_rows, cell_width):
    channels = padded.shape[0]
    term_list = []
    for tap_index in range(9):
        row_off, col_off = divmod(tap_index, 3)
        window = padded[:, row_off : row_off + cell_width, col_off : col_off + cell_width].reshape(
            channels, cell_width * cell_width
        )
        term_list.append(
            lax.dot_general(
                grad_rows, window, (((1,), (1,)), ((), ())), preferred_element_type=jnp.float32
            )
        )
    return jnp.stack(term_list, axis=0)


def body(
    fields,
    conv_a,
    bias_a,
    conv_b,
    cotangent,
    neighbour_tile,
    edge_code,
    corner_tile,
    corner_code,
    corner_missing,
):
    channels = fields.shape[1]
    cell_width = SIDE
    tile_links = (neighbour_tile[0], edge_code[0], corner_tile[0], corner_code[0])
    missing = corner_missing[0]
    field_grid = fields[0].reshape(channels, cell_width, cell_width)
    upstream = cotangent[0]
    back_act = spread_back(upstream, conv_b, cell_width).astype(jnp.bfloat16)
    act_rims, act_rim_corners = rim_payload(back_act, missing)
    (x_picked, x_corners), (ba_picked, ba_corners) = exchange_groups(
        [strip_sides(field_grid), act_rims],
        [corner_cells(field_grid), act_rim_corners],
        tile_links,
    )
    padded_x = assemble_padded(field_grid, x_picked, x_corners, missing)
    pre_act = conv_cells(padded_x, conv_a) + bias_a[:, None]
    activation = jax.nn.gelu(pre_act, approximate=False).astype(jnp.bfloat16)
    pre_saved = pre_act.astype(jnp.bfloat16)
    grad_act = adjoint_sum(back_act, ba_picked, ba_corners)
    grad_pre = (
        grad_act.reshape(channels, cell_width * cell_width)
        * gelu_slope(pre_saved.astype(jnp.float32))
    ).astype(jnp.bfloat16)
    back_x = spread_back(grad_pre, conv_a, cell_width).astype(jnp.bfloat16)
    terms_a = weight_terms(padded_x, grad_pre, cell_width)
    terms_bias = jnp.sum(grad_pre, axis=1, dtype=jnp.float32)
    act_grid = activation.reshape(channels, cell_width, cell_width)
    x_rims, x_rim_corners = rim_payload(back_x, missing)
    (a_picked, a_corners), (bx_picked, bx_corners) = exchange_groups(
        [strip_sides(act_grid), x_rims],
        [corner_cells(act_grid), x_rim_corners],
        tile_links,
    )
    padded_act = assemble_padded(act_grid, a_picked, a_corners, missing)
    output = (fields[0].astype(jnp.float32) + conv_cells(padded_act, conv_b)).astype(jnp.bfloat16)
    terms_b = weight_terms(padded_act, upstream, cell_width)
    tap_size = terms_a.size
    flat = jnp.concatenate([terms_a.reshape(-1), terms_b.reshape(-1), terms_bias])
    summed = tree_all_reduce(flat, HALVING_ROUNDS)
    summed_a = summed[:tap_size].reshape(terms_a.shape)
    summed_b = summed[tap_size : 2 * tap_size].reshape(terms_b.shape)
    summed_bias = summed[2 * tap_size :]
    pulled_x = adjoint_sum(back_x, bx_picked, bx_corners).reshape(
        channels, cell_width * cell_width
    )
    grad_fields = (upstream.astype(jnp.float32) + pulled_x).astype(jnp.bfloat16)
    grad_scale = (lax.axis_size("tiles") * cell_width * cell_width) ** (-0.5)
    return (
        output[None],
        grad_fields[None],
        summed_a * grad_scale,
        summed_b * grad_scale,
        summed_bias * grad_scale,
    )


def solution(mesh):
    return jax.shard_map(
        body,
        mesh=mesh,
        in_specs=(
            P("tiles", None, None),
            P(),
            P(),
            P(),
            P("tiles", None, None),
            P("tiles", None),
            P("tiles", None),
            P("tiles", None),
            P("tiles", None),
            P("tiles", None),
        ),
        out_specs=(P("tiles", None, None), P("tiles", None, None), P(), P(), P()),
        check_vma=False,
    )
```

```python
import jax
import jax.numpy as jnp
from jax import lax
from jax.sharding import PartitionSpec as P

SIDE = 16
TILE_ROW = 8
HALVING_ROUNDS = 3


inv_root_two = 0.7071067811865476
inv_root_tau = 0.3989422804014327


def passed_along(block, axis, distance):
    devices = range(lax.axis_size(axis))
    route = [((i - distance) % len(devices), i) for i in devices]
    return lax.ppermute(block, axis, route)


def xor_partner(block, distance):
    devices = lax.axis_size("tiles")
    return lax.ppermute(block, "tiles", [(i, i ^ distance) for i in range(devices)])


def tree_all_reduce(flat, halving_rounds):
    devices = lax.axis_size("tiles")
    bits = devices.bit_length() - 1
    own = lax.axis_index("tiles")
    halving_rounds = min(halving_rounds, bits)
    quantum = 128 << halving_rounds
    length = flat.shape[0]
    padded = -(-length // quantum) * quantum
    cur = jnp.pad(flat, (0, padded - length))
    for k in range(halving_rounds):
        half = cur.shape[0] // 2
        upper = ((own >> k) & 1) == 1
        low, high = cur[:half], cur[half:]
        keep = jnp.where(upper, high, low)
        send = jnp.where(upper, low, high)
        cur = keep + xor_partner(send, 1 << k)
    for k in range(halving_rounds, bits):
        cur = cur + xor_partner(cur, 1 << k)
    for k in reversed(range(halving_rounds)):
        upper = ((own >> k) & 1) == 1
        got = xor_partner(cur, 1 << k)
        cur = jnp.where(upper, jnp.concatenate([got, cur]), jnp.concatenate([cur, got]))
    return cur[:length]


def paired_shift(block, distance):
    devices = lax.axis_size("tiles")
    own = lax.axis_index("tiles")
    flip = [(i, i ^ distance) for i in range(devices)]
    other = [
        (i, (i + distance) % devices if i & distance else (i - distance) % devices)
        for i in range(devices)
    ]
    got_flip = lax.ppermute(block, "tiles", flip)
    got_other = lax.ppermute(block, "tiles", other)
    low = (own & distance) == 0
    return jnp.where(low, got_flip, got_other), jnp.where(low, got_other, got_flip)


def gelu_slope(values):
    return (
        0.5 * (1.0 + lax.erf(values * inv_root_two))
        + values * jnp.exp(-0.5 * values * values) * inv_root_tau
    )


def strip_sides(tile_field):
    return jnp.stack(
        [tile_field[:, 0, :], tile_field[:, :, -1], tile_field[:, -1, :], tile_field[:, :, 0]],
        axis=0,
    )


def rim_sides(padded):
    return jnp.stack(
        [padded[:, 0, 1:-1], padded[:, 1:-1, -1], padded[:, -1, 1:-1], padded[:, 1:-1, 0]], axis=0
    )


def corner_cells(tile_field):
    return jnp.stack(
        [tile_field[:, 0, 0], tile_field[:, 0, -1], tile_field[:, -1, -1], tile_field[:, -1, 0]],
        axis=0,
    )


def offset_class(linked, offsets):
    device_count = lax.axis_size("tiles")
    own_index = lax.axis_index("tiles")
    relative = (linked - own_index) % device_count
    targets = jnp.array([shift_by % device_count for shift_by in offsets], dtype=jnp.int32)
    matches = (relative[:, None] == targets[None, :]).astype(jnp.int32)
    classes = jnp.sum(matches * jnp.arange(4, dtype=jnp.int32)[None, :], axis=1)
    return (matches, classes)


def corner_row(corners, width):
    block = jnp.transpose(corners, (1, 0))
    block = jnp.pad(block, ((0, 0), (0, width - block.shape[1])))
    return block[None]


def exchange_groups(strip_groups, corner_groups, tile_links):
    neighbour_ids, edge_codes, corner_ids, corner_codes = tile_links
    row_length = TILE_ROW
    edge_offsets = [-row_length, 1, row_length, -1]
    diag_offsets = [1 - row_length, 1 + row_length, row_length - 1, -1 - row_length]
    _, edge_class = offset_class(neighbour_ids, edge_offsets)
    _, diag_class = offset_class(corner_ids, diag_offsets)
    groups = len(strip_groups)
    n_strips = 4 * groups
    strips = jnp.concatenate(strip_groups, axis=0)
    corners = jnp.concatenate(corner_groups, axis=0)
    width = strips.shape[2]
    payload_a = jnp.concatenate([strips, corner_row(corners, width)], axis=0)
    from_next, from_prev = paired_shift(payload_a, 1)
    corners_next = jnp.transpose(from_next[n_strips, :, :n_strips], (1, 0))
    corners_prev = jnp.transpose(from_prev[n_strips, :, :n_strips], (1, 0))
    relay = jnp.concatenate([corners_next, corners_prev], axis=0)
    payload_b = jnp.concatenate([strips, corner_row(relay, width)], axis=0)
    from_down, from_up = paired_shift(payload_b, row_length)
    stacked = jnp.concatenate(
        [from_up[:n_strips], from_next[:n_strips], from_down[:n_strips], from_prev[:n_strips]],
        axis=0,
    )
    up_relay = jnp.transpose(from_up[n_strips, :, : 2 * n_strips], (1, 0))
    down_relay = jnp.transpose(from_down[n_strips, :, : 2 * n_strips], (1, 0))
    corner_stack = jnp.concatenate(
        [up_relay[:n_strips], down_relay[:n_strips], down_relay[n_strips:], up_relay[n_strips:]],
        axis=0,
    )
    reverse = (edge_codes >= 4)[:, None, None]
    their_side = edge_codes % 4
    group_ids = jnp.arange(groups, dtype=jnp.int32)[:, None] * 4
    strip_index = (edge_class * n_strips + their_side)[None, :] + group_ids
    corner_index = (diag_class * n_strips + corner_codes)[None, :] + group_ids
    picked_all = stacked[strip_index.reshape(-1)].reshape((groups, 4) + stacked.shape[1:])
    picked_all = jnp.where(reverse[None], picked_all[..., ::-1], picked_all)
    corner_all = corner_stack[corner_index.reshape(-1)].reshape(
        (groups, 4) + corner_stack.shape[1:]
    )
    return [(picked_all[g], corner_all[g]) for g in range(groups)]


def assemble_padded(tile_field, picked, corner_got, missing):
    corner_got = jnp.where((missing == 1)[:, None], jnp.zeros_like(corner_got), corner_got)
    top = jnp.concatenate(
        [corner_got[0][:, None], picked[0], corner_got[1][:, None]], axis=1
    )
    bottom = jnp.concatenate(
        [corner_got[3][:, None], picked[2], corner_got[2][:, None]], axis=1
    )
    middle = jnp.concatenate(
        [picked[3][:, :, None], tile_field, picked[1][:, :, None]], axis=2
    )
    return jnp.concatenate([top[:, None, :], middle, bottom[:, None, :]], axis=1)


def rim_payload(back_rim, missing):
    rim_corner = corner_cells(back_rim)
    rim_corner = jnp.where((missing == 1)[:, None], jnp.zeros_like(rim_corner), rim_corner)
    return rim_sides(back_rim), rim_corner


def adjoint_sum(back_rim, picked, corner_got):
    summed = back_rim[:, 1:-1, 1:-1].astype(jnp.float32)
    p = picked.astype(jnp.float32)
    c = corner_got.astype(jnp.float32)
    side = SIDE
    summed = summed + jnp.pad(p[0][:, None, :], ((0, 0), (0, side - 1), (0, 0)))
    summed = summed + jnp.pad(p[2][:, None, :], ((0, 0), (side - 1, 0), (0, 0)))
    summed = summed + jnp.pad(p[3][:, :, None], ((0, 0), (0, 0), (0, side - 1)))
    summed = summed + jnp.pad(p[1][:, :, None], ((0, 0), (0, 0), (side - 1, 0)))
    corner_grid = jnp.stack(
        [
            jnp.stack([c[0], c[1]], axis=-1),
            jnp.stack([c[3], c[2]], axis=-1),
        ],
        axis=-2,
    )
    full = lax.pad(corner_grid, jnp.float32(0), ((0, 0, 0), (0, 0, side - 2), (0, 0, side - 2)))
    return summed + full


def conv_cells(padded, weights):
    channels = padded.shape[0]
    cell_width = padded.shape[1] - 2
    windows = jnp.concatenate(
        [
            padded[:, r : r + cell_width, c : c + cell_width].reshape(
                channels, cell_width * cell_width
            )
            for r, c in (divmod(t, 3) for t in range(9))
        ],
        axis=0,
    )
    taps, outs, ins = weights.shape
    flat_weights = jnp.transpose(weights, (1, 0, 2)).reshape(outs, taps * ins)
    return jnp.dot(flat_weights, windows, preferred_element_type=jnp.float32)


def spread_back(grad_rows, weights, cell_width):
    grad_grid = grad_rows.reshape(grad_rows.shape[0], cell_width, cell_width)
    wide_grid = jnp.pad(grad_grid, ((0, 0), (2, 2), (2, 2)))
    ext_width = cell_width + 2
    windows = jnp.concatenate(
        [
            wide_grid[:, 2 - r : 2 - r + ext_width, 2 - c : 2 - c + ext_width].reshape(
                grad_rows.shape[0], ext_width * ext_width
            )
            for r, c in (divmod(t, 3) for t in range(9))
        ],
        axis=0,
    )
    taps, outs, ins = weights.shape
    result = lax.dot_general(
        weights.reshape(taps * outs, ins),
        windows,
        (((0,), (0,)), ((), ())),
        preferred_element_type=jnp.float32,
    )
    return result.reshape(ins, ext_width, ext_width)


def weight_terms(padded, grad_rows, cell_width):
    channels = padded.shape[0]
    term_list = []
    for tap_index in range(9):
        row_off, col_off = divmod(tap_index, 3)
        window = padded[:, row_off : row_off + cell_width, col_off : col_off + cell_width].reshape(
            channels, cell_width * cell_width
        )
        term_list.append(
            lax.dot_general(
                grad_rows, window, (((1,), (1,)), ((), ())), preferred_element_type=jnp.float32
            )
        )
    return jnp.stack(term_list, axis=0)


def body(
    fields,
    conv_a,
    bias_a,
    conv_b,
    cotangent,
    neighbour_tile,
    edge_code,
    corner_tile,
    corner_code,
    corner_missing,
):
    channels = fields.shape[1]
    cell_width = SIDE
    tile_links = (neighbour_tile[0], edge_code[0], corner_tile[0], corner_code[0])
    missing = corner_missing[0]
    field_grid = fields[0].reshape(channels, cell_width, cell_width)
    upstream = cotangent[0]
    back_act = spread_back(upstream, conv_b, cell_width).astype(jnp.bfloat16)
    act_rims, act_rim_corners = rim_payload(back_act, missing)
    (x_picked, x_corners), (ba_picked, ba_corners) = exchange_groups(
        [strip_sides(field_grid), act_rims],
        [corner_cells(field_grid), act_rim_corners],
        tile_links,
    )
    padded_x = assemble_padded(field_grid, x_picked, x_corners, missing)
    pre_act = conv_cells(padded_x, conv_a) + bias_a[:, None]
    activation = jax.nn.gelu(pre_act, approximate=False).astype(jnp.bfloat16)
    pre_saved = pre_act.astype(jnp.bfloat16)
    grad_act = adjoint_sum(back_act, ba_picked, ba_corners)
    grad_pre = (
        grad_act.reshape(channels, cell_width * cell_width)
        * gelu_slope(pre_saved.astype(jnp.float32))
    ).astype(jnp.bfloat16)
    back_x = spread_back(grad_pre, conv_a, cell_width).astype(jnp.bfloat16)
    terms_a = weight_terms(padded_x, grad_pre, cell_width)
    terms_bias = jnp.sum(grad_pre, axis=1, dtype=jnp.float32)
    act_grid = activation.reshape(channels, cell_width, cell_width)
    x_rims, x_rim_corners = rim_payload(back_x, missing)
    (a_picked, a_corners), (bx_picked, bx_corners) = exchange_groups(
        [strip_sides(act_grid), x_rims],
        [corner_cells(act_grid), x_rim_corners],
        tile_links,
    )
    padded_act = assemble_padded(act_grid, a_picked, a_corners, missing)
    output = (fields[0].astype(jnp.float32) + conv_cells(padded_act, conv_b)).astype(jnp.bfloat16)
    terms_b = weight_terms(padded_act, upstream, cell_width)
    tap_size = terms_a.size
    flat = jnp.concatenate([terms_a.reshape(-1), terms_b.reshape(-1), terms_bias])
    summed = tree_all_reduce(flat, HALVING_ROUNDS)
    summed_a = summed[:tap_size].reshape(terms_a.shape)
    summed_b = summed[tap_size : 2 * tap_size].reshape(terms_b.shape)
    summed_bias = summed[2 * tap_size :]
    pulled_x = adjoint_sum(back_x, bx_picked, bx_corners).reshape(
        channels, cell_width * cell_width
    )
    grad_fields = (upstream.astype(jnp.float32) + pulled_x).astype(jnp.bfloat16)
    grad_scale = (lax.axis_size("tiles") * cell_width * cell_width) ** (-0.5)
    return (
        output[None],
        grad_fields[None],
        summed_a * grad_scale,
        summed_b * grad_scale,
        summed_bias * grad_scale,
    )


def solution(mesh):
    return jax.shard_map(
        body,
        mesh=mesh,
        in_specs=(
            P("tiles", None, None),
            P(),
            P(),
            P(),
            P("tiles", None, None),
            P("tiles", None),
            P("tiles", None),
            P("tiles", None),
            P("tiles", None),
            P("tiles", None),
        ),
        out_specs=(P("tiles", None, None), P("tiles", None, None), P(), P(), P()),
        check_vma=False,
    )
```

```python
import jax
import jax.numpy as jnp
from jax import lax
from jax.sharding import PartitionSpec as P

SIDE = 16
TILE_ROW = 8
HALVING_ROUNDS = 3


inv_root_two = 0.7071067811865476
inv_root_tau = 0.3989422804014327


def passed_along(block, axis, distance):
    devices = range(lax.axis_size(axis))
    route = [((i - distance) % len(devices), i) for i in devices]
    return lax.ppermute(block, axis, route)


def xor_partner(block, distance):
    devices = lax.axis_size("tiles")
    return lax.ppermute(block, "tiles", [(i, i ^ distance) for i in range(devices)])


def tree_all_reduce(flat, halving_rounds):
    devices = lax.axis_size("tiles")
    bits = devices.bit_length() - 1
    own = lax.axis_index("tiles")
    halving_rounds = min(halving_rounds, bits)
    quantum = 128 << halving_rounds
    length = flat.shape[0]
    padded = -(-length // quantum) * quantum
    cur = jnp.pad(flat, (0, padded - length))
    for k in range(halving_rounds):
        half = cur.shape[0] // 2
        upper = ((own >> k) & 1) == 1
        low, high = cur[:half], cur[half:]
        keep = jnp.where(upper, high, low)
        send = jnp.where(upper, low, high)
        cur = keep + xor_partner(send, 1 << k)
    for k in range(halving_rounds, bits):
        cur = cur + xor_partner(cur, 1 << k)
    for k in reversed(range(halving_rounds)):
        upper = ((own >> k) & 1) == 1
        got = xor_partner(cur, 1 << k)
        cur = jnp.where(upper, jnp.concatenate([got, cur]), jnp.concatenate([cur, got]))
    return cur[:length]


def paired_shift(block, distance):
    devices = lax.axis_size("tiles")
    own = lax.axis_index("tiles")
    flip = [(i, i ^ distance) for i in range(devices)]
    other = [
        (i, (i + distance) % devices if i & distance else (i - distance) % devices)
        for i in range(devices)
    ]
    got_flip = lax.ppermute(block, "tiles", flip)
    got_other = lax.ppermute(block, "tiles", other)
    low = (own & distance) == 0
    return jnp.where(low, got_flip, got_other), jnp.where(low, got_other, got_flip)


def gelu_slope(values):
    return (
        0.5 * (1.0 + lax.erf(values * inv_root_two))
        + values * jnp.exp(-0.5 * values * values) * inv_root_tau
    )


def strip_sides(tile_field):
    return jnp.stack(
        [tile_field[:, 0, :], tile_field[:, :, -1], tile_field[:, -1, :], tile_field[:, :, 0]],
        axis=0,
    )


def rim_sides(padded):
    return jnp.stack(
        [padded[:, 0, 1:-1], padded[:, 1:-1, -1], padded[:, -1, 1:-1], padded[:, 1:-1, 0]], axis=0
    )


def corner_cells(tile_field):
    return jnp.stack(
        [tile_field[:, 0, 0], tile_field[:, 0, -1], tile_field[:, -1, -1], tile_field[:, -1, 0]],
        axis=0,
    )


def offset_class(linked, offsets):
    device_count = lax.axis_size("tiles")
    own_index = lax.axis_index("tiles")
    relative = (linked - own_index) % device_count
    targets = jnp.array([shift_by % device_count for shift_by in offsets], dtype=jnp.int32)
    matches = (relative[:, None] == targets[None, :]).astype(jnp.int32)
    classes = jnp.sum(matches * jnp.arange(4, dtype=jnp.int32)[None, :], axis=1)
    return (matches, classes)


def corner_row(corners, width):
    block = jnp.transpose(corners, (1, 0))
    block = jnp.pad(block, ((0, 0), (0, width - block.shape[1])))
    return block[None]


def exchange_groups(strip_groups, corner_groups, tile_links):
    neighbour_ids, edge_codes, corner_ids, corner_codes = tile_links
    row_length = TILE_ROW
    edge_offsets = [-row_length, 1, row_length, -1]
    diag_offsets = [1 - row_length, 1 + row_length, row_length - 1, -1 - row_length]
    _, edge_class = offset_class(neighbour_ids, edge_offsets)
    _, diag_class = offset_class(corner_ids, diag_offsets)
    groups = len(strip_groups)
    n_strips = 4 * groups
    strips = jnp.concatenate(strip_groups, axis=0)
    corners = jnp.concatenate(corner_groups, axis=0)
    width = strips.shape[2]
    payload_a = jnp.concatenate([strips, corner_row(corners, width)], axis=0)
    from_next, from_prev = paired_shift(payload_a, 1)
    corners_next = jnp.transpose(from_next[n_strips, :, :n_strips], (1, 0))
    corners_prev = jnp.transpose(from_prev[n_strips, :, :n_strips], (1, 0))
    relay = jnp.concatenate([corners_next, corners_prev], axis=0)
    payload_b = jnp.concatenate([strips, corner_row(relay, width)], axis=0)
    from_down, from_up = paired_shift(payload_b, row_length)
    stacked = jnp.concatenate(
        [from_up[:n_strips], from_next[:n_strips], from_down[:n_strips], from_prev[:n_strips]],
        axis=0,
    )
    up_relay = jnp.transpose(from_up[n_strips, :, : 2 * n_strips], (1, 0))
    down_relay = jnp.transpose(from_down[n_strips, :, : 2 * n_strips], (1, 0))
    corner_stack = jnp.concatenate(
        [up_relay[:n_strips], down_relay[:n_strips], down_relay[n_strips:], up_relay[n_strips:]],
        axis=0,
    )
    reverse = (edge_codes >= 4)[:, None, None]
    their_side = edge_codes % 4
    group_ids = jnp.arange(groups, dtype=jnp.int32)[:, None] * 4
    strip_index = (edge_class * n_strips + their_side)[None, :] + group_ids
    corner_index = (diag_class * n_strips + corner_codes)[None, :] + group_ids
    picked_all = stacked[strip_index.reshape(-1)].reshape((groups, 4) + stacked.shape[1:])
    picked_all = jnp.where(reverse[None], picked_all[..., ::-1], picked_all)
    corner_all = corner_stack[corner_index.reshape(-1)].reshape(
        (groups, 4) + corner_stack.shape[1:]
    )
    return [(picked_all[g], corner_all[g]) for g in range(groups)]


def assemble_padded(tile_field, picked, corner_got, missing):
    corner_got = jnp.where((missing == 1)[:, None], jnp.zeros_like(corner_got), corner_got)
    top = jnp.concatenate(
        [corner_got[0][:, None], picked[0], corner_got[1][:, None]], axis=1
    )
    bottom = jnp.concatenate(
        [corner_got[3][:, None], picked[2], corner_got[2][:, None]], axis=1
    )
    middle = jnp.concatenate(
        [picked[3][:, :, None], tile_field, picked[1][:, :, None]], axis=2
    )
    return jnp.concatenate([top[:, None, :], middle, bottom[:, None, :]], axis=1)


def rim_payload(back_rim, missing):
    rim_corner = corner_cells(back_rim)
    rim_corner = jnp.where((missing == 1)[:, None], jnp.zeros_like(rim_corner), rim_corner)
    return rim_sides(back_rim), rim_corner


def adjoint_sum(back_rim, picked, corner_got):
    summed = back_rim[:, 1:-1, 1:-1].astype(jnp.float32)
    p = picked.astype(jnp.float32)
    c = corner_got.astype(jnp.float32)
    side = SIDE
    summed = summed + jnp.pad(p[0][:, None, :], ((0, 0), (0, side - 1), (0, 0)))
    summed = summed + jnp.pad(p[2][:, None, :], ((0, 0), (side - 1, 0), (0, 0)))
    summed = summed + jnp.pad(p[3][:, :, None], ((0, 0), (0, 0), (0, side - 1)))
    summed = summed + jnp.pad(p[1][:, :, None], ((0, 0), (0, 0), (side - 1, 0)))
    corner_grid = jnp.stack(
        [
            jnp.stack([c[0], c[1]], axis=-1),
            jnp.stack([c[3], c[2]], axis=-1),
        ],
        axis=-2,
    )
    full = lax.pad(corner_grid, jnp.float32(0), ((0, 0, 0), (0, 0, side - 2), (0, 0, side - 2)))
    return summed + full


def conv_cells(padded, weights):
    channels = padded.shape[0]
    cell_width = padded.shape[1] - 2
    windows = jnp.concatenate(
        [
            padded[:, r : r + cell_width, c : c + cell_width].reshape(
                channels, cell_width * cell_width
            )
            for r, c in (divmod(t, 3) for t in range(9))
        ],
        axis=0,
    )
    taps, outs, ins = weights.shape
    flat_weights = jnp.transpose(weights, (1, 0, 2)).reshape(outs, taps * ins)
    return jnp.dot(flat_weights, windows, preferred_element_type=jnp.float32)


def spread_back(grad_rows, weights, cell_width):
    grad_grid = grad_rows.reshape(grad_rows.shape[0], cell_width, cell_width)
    wide_grid = jnp.pad(grad_grid, ((0, 0), (2, 2), (2, 2)))
    ext_width = cell_width + 2
    windows = jnp.concatenate(
        [
            wide_grid[:, 2 - r : 2 - r + ext_width, 2 - c : 2 - c + ext_width].reshape(
                grad_rows.shape[0], ext_width * ext_width
            )
            for r, c in (divmod(t, 3) for t in range(9))
        ],
        axis=0,
    )
    taps, outs, ins = weights.shape
    result = lax.dot_general(
        weights.reshape(taps * outs, ins),
        windows,
        (((0,), (0,)), ((), ())),
        preferred_element_type=jnp.float32,
    )
    return result.reshape(ins, ext_width, ext_width)


def weight_terms(padded, grad_rows, cell_width):
    channels = padded.shape[0]
    windows = jnp.concatenate(
        [
            padded[:, r : r + cell_width, c : c + cell_width].reshape(
                channels, cell_width * cell_width
            )
            for r, c in (divmod(t, 3) for t in range(9))
        ],
        axis=0,
    )
    terms = lax.dot_general(
        grad_rows, windows, (((1,), (1,)), ((), ())), preferred_element_type=jnp.float32
    )
    return jnp.transpose(terms.reshape(grad_rows.shape[0], 9, channels), (1, 0, 2))


def body(
    fields,
    conv_a,
    bias_a,
    conv_b,
    cotangent,
    neighbour_tile,
    edge_code,
    corner_tile,
    corner_code,
    corner_missing,
):
    channels = fields.shape[1]
    cell_width = SIDE
    tile_links = (neighbour_tile[0], edge_code[0], corner_tile[0], corner_code[0])
    missing = corner_missing[0]
    field_grid = fields[0].reshape(channels, cell_width, cell_width)
    upstream = cotangent[0]
    back_act = spread_back(upstream, conv_b, cell_width).astype(jnp.bfloat16)
    act_rims, act_rim_corners = rim_payload(back_act, missing)
    (x_picked, x_corners), (ba_picked, ba_corners) = exchange_groups(
        [strip_sides(field_grid), act_rims],
        [corner_cells(field_grid), act_rim_corners],
        tile_links,
    )
    padded_x = assemble_padded(field_grid, x_picked, x_corners, missing)
    pre_act = conv_cells(padded_x, conv_a) + bias_a[:, None]
    activation = jax.nn.gelu(pre_act, approximate=False).astype(jnp.bfloat16)
    pre_saved = pre_act.astype(jnp.bfloat16)
    grad_act = adjoint_sum(back_act, ba_picked, ba_corners)
    grad_pre = (
        grad_act.reshape(channels, cell_width * cell_width)
        * gelu_slope(pre_saved.astype(jnp.float32))
    ).astype(jnp.bfloat16)
    back_x = spread_back(grad_pre, conv_a, cell_width).astype(jnp.bfloat16)
    terms_a = weight_terms(padded_x, grad_pre, cell_width)
    terms_bias = jnp.sum(grad_pre, axis=1, dtype=jnp.float32)
    act_grid = activation.reshape(channels, cell_width, cell_width)
    x_rims, x_rim_corners = rim_payload(back_x, missing)
    (a_picked, a_corners), (bx_picked, bx_corners) = exchange_groups(
        [strip_sides(act_grid), x_rims],
        [corner_cells(act_grid), x_rim_corners],
        tile_links,
    )
    padded_act = assemble_padded(act_grid, a_picked, a_corners, missing)
    output = (fields[0].astype(jnp.float32) + conv_cells(padded_act, conv_b)).astype(jnp.bfloat16)
    terms_b = weight_terms(padded_act, upstream, cell_width)
    tap_size = terms_a.size
    flat = jnp.concatenate([terms_a.reshape(-1), terms_b.reshape(-1), terms_bias])
    summed = tree_all_reduce(flat, HALVING_ROUNDS)
    summed_a = summed[:tap_size].reshape(terms_a.shape)
    summed_b = summed[tap_size : 2 * tap_size].reshape(terms_b.shape)
    summed_bias = summed[2 * tap_size :]
    pulled_x = adjoint_sum(back_x, bx_picked, bx_corners).reshape(
        channels, cell_width * cell_width
    )
    grad_fields = (upstream.astype(jnp.float32) + pulled_x).astype(jnp.bfloat16)
    grad_scale = (lax.axis_size("tiles") * cell_width * cell_width) ** (-0.5)
    return (
        output[None],
        grad_fields[None],
        summed_a * grad_scale,
        summed_b * grad_scale,
        summed_bias * grad_scale,
    )


def solution(mesh):
    return jax.shard_map(
        body,
        mesh=mesh,
        in_specs=(
            P("tiles", None, None),
            P(),
            P(),
            P(),
            P("tiles", None, None),
            P("tiles", None),
            P("tiles", None),
            P("tiles", None),
            P("tiles", None),
            P("tiles", None),
        ),
        out_specs=(P("tiles", None, None), P("tiles", None, None), P(), P(), P()),
        check_vma=False,
    )
```

```python
import jax
import jax.numpy as jnp
from jax import lax
from jax.sharding import PartitionSpec as P

SIDE = 16
TILE_ROW = 8
HALVING_ROUNDS = 3


inv_root_two = 0.7071067811865476
inv_root_tau = 0.3989422804014327


def passed_along(block, axis, distance):
    devices = range(lax.axis_size(axis))
    route = [((i - distance) % len(devices), i) for i in devices]
    return lax.ppermute(block, axis, route)


def xor_partner(block, distance):
    devices = lax.axis_size("tiles")
    return lax.ppermute(block, "tiles", [(i, i ^ distance) for i in range(devices)])


def tree_all_reduce(flat, halving_rounds):
    devices = lax.axis_size("tiles")
    bits = devices.bit_length() - 1
    own = lax.axis_index("tiles")
    halving_rounds = min(halving_rounds, bits)
    quantum = 128 << halving_rounds
    length = flat.shape[0]
    padded = -(-length // quantum) * quantum
    cur = jnp.pad(flat, (0, padded - length))
    for k in range(halving_rounds):
        half = cur.shape[0] // 2
        upper = ((own >> k) & 1) == 1
        low, high = cur[:half], cur[half:]
        keep = jnp.where(upper, high, low)
        send = jnp.where(upper, low, high)
        cur = keep + xor_partner(send, 1 << k)
    for k in range(halving_rounds, bits):
        cur = cur + xor_partner(cur, 1 << k)
    for k in reversed(range(halving_rounds)):
        upper = ((own >> k) & 1) == 1
        got = xor_partner(cur, 1 << k)
        cur = jnp.where(upper, jnp.concatenate([got, cur]), jnp.concatenate([cur, got]))
    return cur[:length]


def paired_shift(block, distance):
    devices = lax.axis_size("tiles")
    own = lax.axis_index("tiles")
    flip = [(i, i ^ distance) for i in range(devices)]
    other = [
        (i, (i + distance) % devices if i & distance else (i - distance) % devices)
        for i in range(devices)
    ]
    got_flip = lax.ppermute(block, "tiles", flip)
    got_other = lax.ppermute(block, "tiles", other)
    low = (own & distance) == 0
    return jnp.where(low, got_flip, got_other), jnp.where(low, got_other, got_flip)


def gelu_slope(values):
    return (
        0.5 * (1.0 + lax.erf(values * inv_root_two))
        + values * jnp.exp(-0.5 * values * values) * inv_root_tau
    )


def strip_sides(tile_field):
    return jnp.stack(
        [tile_field[:, 0, :], tile_field[:, :, -1], tile_field[:, -1, :], tile_field[:, :, 0]],
        axis=0,
    )


def rim_sides(padded):
    return jnp.stack(
        [padded[:, 0, 1:-1], padded[:, 1:-1, -1], padded[:, -1, 1:-1], padded[:, 1:-1, 0]], axis=0
    )


def corner_cells(tile_field):
    return jnp.stack(
        [tile_field[:, 0, 0], tile_field[:, 0, -1], tile_field[:, -1, -1], tile_field[:, -1, 0]],
        axis=0,
    )


def offset_class(linked, offsets):
    device_count = lax.axis_size("tiles")
    own_index = lax.axis_index("tiles")
    relative = (linked - own_index) % device_count
    targets = jnp.array([shift_by % device_count for shift_by in offsets], dtype=jnp.int32)
    matches = (relative[:, None] == targets[None, :]).astype(jnp.int32)
    classes = jnp.sum(matches * jnp.arange(4, dtype=jnp.int32)[None, :], axis=1)
    return (matches, classes)


def corner_row(corners, width):
    block = jnp.transpose(corners, (1, 0))
    block = jnp.pad(block, ((0, 0), (0, width - block.shape[1])))
    return block[None]


def exchange_groups(strip_groups, corner_groups, tile_links):
    neighbour_ids, edge_codes, corner_ids, corner_codes = tile_links
    row_length = TILE_ROW
    edge_offsets = [-row_length, 1, row_length, -1]
    diag_offsets = [1 - row_length, 1 + row_length, row_length - 1, -1 - row_length]
    _, edge_class = offset_class(neighbour_ids, edge_offsets)
    _, diag_class = offset_class(corner_ids, diag_offsets)
    groups = len(strip_groups)
    n_strips = 4 * groups
    strips = jnp.concatenate(strip_groups, axis=0)
    corners = jnp.concatenate(corner_groups, axis=0)
    width = strips.shape[2]
    payload_a = jnp.concatenate([strips, corner_row(corners, width)], axis=0)
    from_next, from_prev = paired_shift(payload_a, 1)
    corners_next = jnp.transpose(from_next[n_strips, :, :n_strips], (1, 0))
    corners_prev = jnp.transpose(from_prev[n_strips, :, :n_strips], (1, 0))
    relay = jnp.concatenate([corners_next, corners_prev], axis=0)
    payload_b = jnp.concatenate([strips, corner_row(relay, width)], axis=0)
    from_down, from_up = paired_shift(payload_b, row_length)
    stacked = jnp.concatenate(
        [from_up[:n_strips], from_next[:n_strips], from_down[:n_strips], from_prev[:n_strips]],
        axis=0,
    )
    up_relay = jnp.transpose(from_up[n_strips, :, : 2 * n_strips], (1, 0))
    down_relay = jnp.transpose(from_down[n_strips, :, : 2 * n_strips], (1, 0))
    corner_stack = jnp.concatenate(
        [up_relay[:n_strips], down_relay[:n_strips], down_relay[n_strips:], up_relay[n_strips:]],
        axis=0,
    )
    reverse = (edge_codes >= 4)[:, None, None]
    their_side = edge_codes % 4
    group_ids = jnp.arange(groups, dtype=jnp.int32)[:, None] * 4
    strip_index = (edge_class * n_strips + their_side)[None, :] + group_ids
    corner_index = (diag_class * n_strips + corner_codes)[None, :] + group_ids
    picked_all = stacked[strip_index.reshape(-1)].reshape((groups, 4) + stacked.shape[1:])
    picked_all = jnp.where(reverse[None], picked_all[..., ::-1], picked_all)
    corner_all = corner_stack[corner_index.reshape(-1)].reshape(
        (groups, 4) + corner_stack.shape[1:]
    )
    return [(picked_all[g], corner_all[g]) for g in range(groups)]


def assemble_padded(tile_field, picked, corner_got, missing):
    corner_got = jnp.where((missing == 1)[:, None], jnp.zeros_like(corner_got), corner_got)
    top = jnp.concatenate(
        [corner_got[0][:, None], picked[0], corner_got[1][:, None]], axis=1
    )
    bottom = jnp.concatenate(
        [corner_got[3][:, None], picked[2], corner_got[2][:, None]], axis=1
    )
    middle = jnp.concatenate(
        [picked[3][:, :, None], tile_field, picked[1][:, :, None]], axis=2
    )
    return jnp.concatenate([top[:, None, :], middle, bottom[:, None, :]], axis=1)


def rim_payload(back_rim, missing):
    rim_corner = corner_cells(back_rim)
    rim_corner = jnp.where((missing == 1)[:, None], jnp.zeros_like(rim_corner), rim_corner)
    return rim_sides(back_rim), rim_corner


def adjoint_sum(back_rim, picked, corner_got):
    summed = back_rim[:, 1:-1, 1:-1].astype(jnp.float32)
    p = picked.astype(jnp.float32)
    c = corner_got.astype(jnp.float32)
    side = SIDE
    summed = summed + jnp.pad(p[0][:, None, :], ((0, 0), (0, side - 1), (0, 0)))
    summed = summed + jnp.pad(p[2][:, None, :], ((0, 0), (side - 1, 0), (0, 0)))
    summed = summed + jnp.pad(p[3][:, :, None], ((0, 0), (0, 0), (0, side - 1)))
    summed = summed + jnp.pad(p[1][:, :, None], ((0, 0), (0, 0), (side - 1, 0)))
    corner_grid = jnp.stack(
        [
            jnp.stack([c[0], c[1]], axis=-1),
            jnp.stack([c[3], c[2]], axis=-1),
        ],
        axis=-2,
    )
    full = lax.pad(corner_grid, jnp.float32(0), ((0, 0, 0), (0, 0, side - 2), (0, 0, side - 2)))
    return summed + full


def conv_cells(padded, weights):
    channels = padded.shape[0]
    cell_width = padded.shape[1] - 2
    windows = jnp.concatenate(
        [
            padded[:, r : r + cell_width, c : c + cell_width].reshape(
                channels, cell_width * cell_width
            )
            for r, c in (divmod(t, 3) for t in range(9))
        ],
        axis=0,
    )
    taps, outs, ins = weights.shape
    flat_weights = jnp.transpose(weights, (1, 0, 2)).reshape(outs, taps * ins)
    return jnp.dot(flat_weights, windows, preferred_element_type=jnp.float32)


def spread_back(grad_rows, weights, cell_width):
    grad_grid = grad_rows.reshape(grad_rows.shape[0], cell_width, cell_width)
    wide_grid = jnp.pad(grad_grid, ((0, 0), (2, 2), (2, 2)))
    ext_width = cell_width + 2
    windows = jnp.concatenate(
        [
            wide_grid[:, 2 - r : 2 - r + ext_width, 2 - c : 2 - c + ext_width].reshape(
                grad_rows.shape[0], ext_width * ext_width
            )
            for r, c in (divmod(t, 3) for t in range(9))
        ],
        axis=0,
    )
    taps, outs, ins = weights.shape
    result = lax.dot_general(
        weights.reshape(taps * outs, ins),
        windows,
        (((0,), (0,)), ((), ())),
        preferred_element_type=jnp.float32,
    )
    return result.reshape(ins, ext_width, ext_width)


def weight_terms(padded, grad_rows, cell_width):
    channels = padded.shape[0]
    term_list = []
    for tap_index in range(9):
        row_off, col_off = divmod(tap_index, 3)
        window = padded[:, row_off : row_off + cell_width, col_off : col_off + cell_width].reshape(
            channels, cell_width * cell_width
        )
        term_list.append(
            lax.dot_general(
                grad_rows, window, (((1,), (1,)), ((), ())), preferred_element_type=jnp.float32
            )
        )
    return jnp.stack(term_list, axis=0)


def body(
    fields,
    conv_a,
    bias_a,
    conv_b,
    cotangent,
    neighbour_tile,
    edge_code,
    corner_tile,
    corner_code,
    corner_missing,
):
    channels = fields.shape[1]
    cell_width = SIDE
    tile_links = (neighbour_tile[0], edge_code[0], corner_tile[0], corner_code[0])
    missing = corner_missing[0]
    field_grid = fields[0].reshape(channels, cell_width, cell_width)
    upstream = cotangent[0]
    back_act = spread_back(upstream, conv_b, cell_width).astype(jnp.bfloat16)
    act_rims, act_rim_corners = rim_payload(back_act, missing)
    (x_picked, x_corners), (ba_picked, ba_corners) = exchange_groups(
        [strip_sides(field_grid), act_rims],
        [corner_cells(field_grid), act_rim_corners],
        tile_links,
    )
    padded_x = assemble_padded(field_grid, x_picked, x_corners, missing)
    pre_act = conv_cells(padded_x, conv_a) + bias_a[:, None]
    activation = jax.nn.gelu(pre_act, approximate=False).astype(jnp.bfloat16)
    pre_saved = pre_act.astype(jnp.bfloat16)
    grad_act = adjoint_sum(back_act, ba_picked, ba_corners)
    grad_pre = (
        grad_act.reshape(channels, cell_width * cell_width)
        * gelu_slope(pre_saved.astype(jnp.float32))
    ).astype(jnp.bfloat16)
    back_x = spread_back(grad_pre, conv_a, cell_width).astype(jnp.bfloat16)
    terms_a = weight_terms(padded_x, grad_pre, cell_width)
    terms_bias = jnp.sum(grad_pre, axis=1, dtype=jnp.float32)
    act_grid = activation.reshape(channels, cell_width, cell_width)
    x_rims, x_rim_corners = rim_payload(back_x, missing)
    (a_picked, a_corners), (bx_picked, bx_corners) = exchange_groups(
        [strip_sides(act_grid), x_rims],
        [corner_cells(act_grid), x_rim_corners],
        tile_links,
    )
    padded_act = assemble_padded(act_grid, a_picked, a_corners, missing)
    output = (fields[0].astype(jnp.float32) + conv_cells(padded_act, conv_b)).astype(jnp.bfloat16)
    terms_b = weight_terms(padded_act, upstream, cell_width)
    tap_size = terms_a.size
    grad_scale = (lax.axis_size("tiles") * cell_width * cell_width) ** (-0.5)
    flat = jnp.concatenate([terms_a.reshape(-1), terms_b.reshape(-1), terms_bias]) * grad_scale
    summed = tree_all_reduce(flat, HALVING_ROUNDS)
    summed_a = summed[:tap_size].reshape(terms_a.shape)
    summed_b = summed[tap_size : 2 * tap_size].reshape(terms_b.shape)
    summed_bias = summed[2 * tap_size :]
    pulled_x = adjoint_sum(back_x, bx_picked, bx_corners).reshape(
        channels, cell_width * cell_width
    )
    grad_fields = (upstream.astype(jnp.float32) + pulled_x).astype(jnp.bfloat16)
    return (output[None], grad_fields[None], summed_a, summed_b, summed_bias)


def solution(mesh):
    return jax.shard_map(
        body,
        mesh=mesh,
        in_specs=(
            P("tiles", None, None),
            P(),
            P(),
            P(),
            P("tiles", None, None),
            P("tiles", None),
            P("tiles", None),
            P("tiles", None),
            P("tiles", None),
            P("tiles", None),
        ),
        out_specs=(P("tiles", None, None), P("tiles", None, None), P(), P(), P()),
        check_vma=False,
    )
```
